32 devices in a mesh: seq: 8 (over y, x, core), panel: 4 (over z).
Axes of the slice: x: 2, y: 2, z: 4, core: 2. Of those that a mesh axis runs over, the one named last changes fastest.
Arguments:
- tokens: bfloat16 [2048, 1024], P('seq', 'panel'), may hold values from -6 to 6
- cotangent: bfloat16 [2048, 1024], P('seq', 'panel'), may hold values from -6 to 6
- in_weight: bfloat16 [3, 1024, 1024], P(None, None, 'panel'), may hold values from -0.1875 to 0.1875
- short_kernel: float32 [3, 3, 1024], P(None, None, 'panel'), may hold values from -1 to 1
- skip_gain: float32 [1024], P('panel'), may hold values from 0.5 to 1.5
- long_filter: float32 [2048, 1024], P('seq', 'panel'), may hold values from -1.25 to 1.25
- out_weight: bfloat16 [1024, 1024], P('panel'), may hold values from -0.1875 to 0.1875
Outputs:
- block_out: bfloat16 [2048, 1024], P('seq', 'panel')
- token_grad: bfloat16 [2048, 1024], P('seq', 'panel')
The draws below stay inside these ranges and needn't reach their ends.
All inputs are finite; a program needn't handle non-finite values.
Results may differ from the reference program's by a relative error of at most 0.007.
Values may be sent and summed in bfloat16 or wider, within the bound.
No kernel may reach another device: no remote copies, remote signals or barrier semaphores. Data moves between devices by JAX's collectives and lax.ppermute only.
A program may use at most 64 MiB of HBM per device.

```python
import math
import jax
import jax.numpy as jnp
from jax import lax

D = 1024
SHORT = 3
SEQ = 2048


def draw_long_filter(key, part):
    rate_key, noise_key, slow_key, tail_key = jax.random.split(jax.random.fold_in(key, 17), 4)
    rate_low, rate_high = (0.3, SEQ / 30.0)
    decay_rates = jnp.exp(jax.random.uniform(rate_key, (D,), jnp.float32, math.log(rate_low), math.log(rate_high)))
    position = jnp.arange(SEQ, dtype=jnp.float32)[:, None]
    envelope = jnp.exp(-decay_rates[None, :] * position / SEQ) * jnp.sqrt(2.0 * decay_rates / SEQ)[None, :]
    noise_part = jax.random.truncated_normal(noise_key, -4.0, 4.0, (SEQ, D), jnp.float32)
    slow_rates = jnp.exp(jax.random.uniform(slow_key, (D,), jnp.float32, math.log(0.2), math.log(1.0)))
    slow_norm = jnp.sqrt(2.0 * slow_rates / SEQ / (1.0 - jnp.exp(-2.0 * slow_rates)))
    slow_envelope = jnp.exp(-slow_rates[None, :] * position / SEQ) * slow_norm[None, :]
    tail_noise = jax.random.truncated_normal(tail_key, -4.0, 4.0, (SEQ, D), jnp.float32)
    return noise_part * envelope + 0.3 * tail_noise * slow_envelope


def block_levels(stream_key, shape, shards, least, top_value):
    def one(axis_at, shards_of):
        steps = jax.random.uniform(jax.random.fold_in(jax.random.fold_in(stream_key, 6), axis_at), (shards_of,), jnp.float32, least / len(shards), top_value / len(shards))
        return jnp.repeat(jnp.exp(steps), shape[axis_at] // shards_of).reshape((-1,) + (1,) * (len(shape) - axis_at - 1))

    loudness = one(*shards[0])
    for cut in shards[1:]:
        loudness = loudness * one(*cut)
    return loudness


def normal_values(stream_key, dims, scale, bound, shards=(), held_as=jnp.bfloat16):
    values = scale * jax.random.normal(stream_key, dims, jnp.float32)
    if shards:
        values = values * block_levels(stream_key, dims, shards, -0.22, 0.18)
    return jnp.clip(values, -bound, bound).astype(held_as)


def setup_inputs(seed: int = 0) -> dict:
    streams_of = jax.random.split(jax.random.key(seed), 8)
    return {
        "tokens": normal_values(streams_of[0], (SEQ, D), 1.0, 6.0, ((0, 8), (1, 4))),
        "cotangent": normal_values(streams_of[1], (SEQ, D), 1.0, 6.0, ((0, 8), (1, 4))),
        "in_weight": normal_values(streams_of[2], (3, D, D), D ** -0.5, 0.1875, ((2, 4),)),
        "short_kernel": jnp.clip(jax.random.uniform(streams_of[3], (SHORT, 3, D), jnp.float32, -1.0, 1.0) * block_levels(streams_of[3], (SHORT, 3, D), ((2, 4),), -0.4, 0.0), -1.0, 1.0),
        "skip_gain": jnp.clip(0.5 + 1.0 * jax.random.uniform(streams_of[4], (D,), jnp.float32) ** block_levels(streams_of[4], (D,), ((0, 4),), -0.2, 0.2), 0.5, 1.5),
        "long_filter": draw_long_filter(jax.random.fold_in(streams_of[7], 71), 0),
        "out_weight": normal_values(streams_of[6], (D, D), D ** -0.5, 0.1875, ((0, 4),)),
    }


def causal_short(projected, short_kernel):
    tap_count = short_kernel.shape[0]
    filtered = short_kernel[0][:, None, :] * projected
    for tap_index in range(1, tap_count):
        shifted = jnp.pad(projected[:, :-tap_index, :], ((0, 0), (tap_index, 0), (0, 0)))
        filtered = filtered + short_kernel[tap_index][:, None, :] * shifted
    return filtered


def anticausal_short(upstream, short_kernel):
    tap_count = short_kernel.shape[0]
    result = short_kernel[0][:, None, :] * upstream
    for tap_index in range(1, tap_count):
        shifted = jnp.pad(upstream[:, tap_index:, :], ((0, 0), (0, tap_index), (0, 0)))
        result = result + short_kernel[tap_index][:, None, :] * shifted
    return result


def long_conv(signal, long_filter, mirror):
    block_width = math.gcd(D, 128)
    groups = D // block_width
    sig_blocks = signal.reshape(SEQ, groups, block_width).transpose(1, 0, 2)
    fil_blocks = long_filter.reshape(SEQ, groups, block_width).transpose(1, 0, 2)

    def one_block(operands):
        sig_part, fil_part = operands
        sig_freq = jnp.fft.rfft(sig_part, n=2 * SEQ, axis=0)
        fil_freq = jnp.fft.rfft(fil_part, n=2 * SEQ, axis=0)
        if mirror:
            fil_freq = jnp.conj(fil_freq)
        return jnp.fft.irfft(sig_freq * fil_freq, n=2 * SEQ, axis=0)[:SEQ]

    result = lax.map(one_block, (sig_blocks, fil_blocks))
    return result.transpose(1, 0, 2).reshape(SEQ, D)


def reference(tokens, cotangent, in_weight, short_kernel, skip_gain, long_filter, out_weight):
    projected = jnp.stack([jnp.dot(tokens, in_weight[branch], preferred_element_type=jnp.float32) for branch in range(3)]).astype(jnp.bfloat16)
    filtered = causal_short(projected.astype(jnp.float32), short_kernel)
    gate_out, gate_in, value_path = filtered[0], filtered[1], filtered[2]
    signal = value_path * gate_in
    conv_state = long_conv(signal, long_filter, False) + skip_gain[None, :] * signal
    gated_state = (conv_state * gate_out).astype(jnp.bfloat16)
    block_out = jnp.dot(gated_state, out_weight, preferred_element_type=jnp.float32).astype(jnp.bfloat16)
    grad_gated = jnp.dot(cotangent, out_weight.T, preferred_element_type=jnp.float32)
    grad_gate_out = grad_gated * conv_state
    grad_state = grad_gated * gate_out
    grad_signal = long_conv(grad_state, long_filter, True) + skip_gain[None, :] * grad_state
    grad_value = grad_signal * gate_in
    grad_gate_in = grad_signal * value_path
    upstream = jnp.stack([grad_gate_out, grad_gate_in, grad_value])
    grad_projected = anticausal_short(upstream, short_kernel).astype(jnp.bfloat16)
    token_grad = jnp.dot(grad_projected[0], in_weight[0].T, preferred_element_type=jnp.float32)
    for branch in range(1, 3):
        token_grad = token_grad + jnp.dot(grad_projected[branch], in_weight[branch].T, preferred_element_type=jnp.float32)
    return block_out, token_grad.astype(jnp.bfloat16)
```

```python
import math

import jax
import jax.numpy as jnp
from jax import lax
from jax.sharding import PartitionSpec as P

HIGHEST = lax.Precision.HIGHEST
STAGE_A_PRECISION = lax.Precision.HIGHEST
STAGE_B_PRECISION = lax.Precision.HIGHEST


def shifted(value, axis, steps):
    count = lax.axis_size(axis)
    initial, last = (max(0, -steps), min(count, count - steps))
    return lax.ppermute(value, axis, [(source, source + steps) for source in range(initial, last)])


def phase(numer, period):
    return (2.0 * math.pi / period) * (numer % period).astype(jnp.float32)


def transform_tables(shard_count, row_count):
    length = shard_count * row_count
    branch = jnp.arange(2, dtype=jnp.int32)
    shard = jnp.arange(shard_count, dtype=jnp.int32)
    row = jnp.arange(row_count, dtype=jnp.int32)
    theta = -phase(
        (2 * shard[:, None] * shard[None, :])[None] + branch[:, None, None] * shard[None, None, :],
        2 * shard_count,
    )
    stage_a = jnp.stack([jnp.cos(theta), jnp.sin(theta)], axis=1)
    phi = -phase(
        (2 * shard[:, None] * row[None, :])[None] + branch[:, None, None] * row[None, :][None],
        2 * length,
    )
    twiddle = (jnp.cos(phi), jnp.sin(phi))
    psi = -phase(row[:, None] * row[None, :], row_count)
    cos_b, sin_b = jnp.cos(psi), jnp.sin(psi)
    stage_b = jnp.stack(
        [jnp.stack([cos_b, sin_b], axis=1), jnp.stack([-sin_b, cos_b], axis=1)]
    )
    stage_b_inv = jnp.stack(
        [jnp.stack([cos_b, -sin_b], axis=1), jnp.stack([sin_b, cos_b], axis=1)]
    )
    stage_a_inv = stage_a * (0.5 / length)
    return stage_a, twiddle, stage_b, stage_b_inv, stage_a_inv


def complex_scale(value, cos_part, sin_part, axis):
    real_part = lax.index_in_dim(value, 0, axis, keepdims=False)
    imag_part = lax.index_in_dim(value, 1, axis, keepdims=False)
    return jnp.stack(
        [real_part * cos_part - imag_part * sin_part, real_part * sin_part + imag_part * cos_part],
        axis=axis,
    )


def to_columns(rows):
    shard_count = lax.axis_size("seq")
    batch, row_count, _ = rows.shape
    columns = lax.all_to_all(
        jnp.swapaxes(rows, 1, 2), "seq", split_axis=1, concat_axis=2, tiled=True
    )
    return columns.reshape(batch, columns.shape[1], shard_count, row_count)


def to_rows(columns):
    batch, chan_count, shard_count, row_count = columns.shape
    flat = columns.reshape(batch, chan_count, shard_count * row_count)
    rows = lax.all_to_all(flat, "seq", split_axis=2, concat_axis=1, tiled=True)
    return jnp.swapaxes(rows, 1, 2)


def forward_spectrum(columns, tables):
    stage_a, twiddle, stage_b, _, _ = tables
    spread = jnp.einsum("erkp,bcpm->bcerkm", stage_a, columns, precision=STAGE_A_PRECISION)
    spread = complex_scale(spread, twiddle[0], twiddle[1], 3)
    return jnp.einsum("bcerkm,rmsq->bceskq", spread, stage_b, precision=STAGE_B_PRECISION)


def inverse_spectrum(spectrum, tables):
    _, twiddle, _, stage_b_inv, stage_a_inv = tables
    spread = jnp.einsum("bceskq,sqrm->bcerkm", spectrum, stage_b_inv, precision=STAGE_B_PRECISION)
    spread = complex_scale(spread, twiddle[0], -twiddle[1], 3)
    return jnp.einsum("erkp,bcerkm->bcpm", stage_a_inv, spread, precision=STAGE_A_PRECISION)


def local(tokens, cotangent, in_weight, short_kernel, skip_gain, long_filter, out_weight):
    row_count = tokens.shape[0]
    tap_count = short_kernel.shape[0]
    shard_count = lax.axis_size("seq")
    tables = transform_tables(shard_count, row_count)
    filt_spec = forward_spectrum(to_columns(long_filter[None]), tables)
    both = lax.all_gather(
        jnp.concatenate([tokens, cotangent], axis=0), "panel", axis=1, tiled=True
    )
    full_tok, full_cot = both[:row_count], both[row_count:]
    projected = jnp.einsum(
        "td,jdc->jtc", full_tok, in_weight, preferred_element_type=jnp.float32
    ).astype(jnp.bfloat16)
    before = shifted(projected[:, row_count - (tap_count - 1) :, :], "seq", 1)
    extended = jnp.concatenate([before, projected], axis=1).astype(jnp.float32)
    filtered = short_kernel[0][:, None, :] * extended[:, tap_count - 1 :, :]
    for tap_index in range(1, tap_count):
        filtered = (
            filtered
            + short_kernel[tap_index][:, None, :]
            * extended[:, tap_count - 1 - tap_index : tap_count - 1 - tap_index + row_count, :]
        )
    gate_out, gate_in, value_path = (filtered[0], filtered[1], filtered[2])
    signal = value_path * gate_in
    grad_gated = lax.dot_general(
        full_cot, out_weight, (((1,), (1,)), ((), ())), preferred_element_type=jnp.float32
    )
    grad_state = grad_gated * gate_out
    spectra = forward_spectrum(to_columns(jnp.stack([signal, grad_state])), tables)
    filt_real, filt_imag = filt_spec[:, :, :, 0], filt_spec[:, :, :, 1]
    sig_real, sig_imag = spectra[0:1, :, :, 0], spectra[0:1, :, :, 1]
    grad_real, grad_imag = spectra[1:2, :, :, 0], spectra[1:2, :, :, 1]
    product = jnp.concatenate(
        [
            jnp.stack(
                [sig_real * filt_real - sig_imag * filt_imag, sig_real * filt_imag + sig_imag * filt_real],
                axis=3,
            ),
            jnp.stack(
                [grad_real * filt_real + grad_imag * filt_imag, grad_imag * filt_real - grad_real * filt_imag],
                axis=3,
            ),
        ]
    )
    convolved = to_rows(inverse_spectrum(product, tables))
    conv_state = convolved[0] + skip_gain[None, :] * signal
    grad_signal = convolved[1] + skip_gain[None, :] * grad_state
    gated_state = (conv_state * gate_out).astype(jnp.bfloat16)
    partial_value = jnp.dot(gated_state, out_weight, preferred_element_type=jnp.float32)
    block_out = lax.psum_scatter(partial_value, "panel", scatter_dimension=1, tiled=True).astype(
        jnp.bfloat16
    )
    grad_gate_out = grad_gated * conv_state
    grad_value = grad_signal * gate_in
    grad_gate_in = grad_signal * value_path
    upstream = jnp.stack([grad_gate_out, grad_gate_in, grad_value])
    after_rim = shifted(upstream[:, : tap_count - 1, :], "seq", -1)
    widened = jnp.concatenate([upstream, after_rim], axis=1)
    grad_projected = short_kernel[0][:, None, :] * widened[:, :row_count, :]
    for tap_index in range(1, tap_count):
        grad_projected = (
            grad_projected
            + short_kernel[tap_index][:, None, :] * widened[:, tap_index : tap_index + row_count, :]
        )
    grad_projected = grad_projected.astype(jnp.bfloat16)
    grad_partial = jnp.einsum(
        "jtc,jdc->td", grad_projected, in_weight, preferred_element_type=jnp.float32
    )
    token_grad = lax.psum_scatter(grad_partial, "panel", scatter_dimension=1, tiled=True).astype(
        jnp.bfloat16
    )
    return (block_out, token_grad)


def solution(mesh):
    placed = (
        P("seq", "panel"),
        P("seq", "panel"),
        P(None, None, "panel"),
        P(None, None, "panel"),
        P("panel"),
        P("seq", "panel"),
        P("panel", None),
    )
    return jax.shard_map(
        local,
        mesh=mesh,
        in_specs=placed,
        out_specs=(P("seq", "panel"), P("seq", "panel")),
        check_vma=False,
    )
```

```python
import math

import jax
import jax.numpy as jnp
from jax import lax
from jax.sharding import PartitionSpec as P

HIGHEST = lax.Precision.HIGHEST
STAGE_A_PRECISION = lax.Precision.HIGHEST
STAGE_B_PRECISION = lax.Precision.HIGH


def shifted(value, axis, steps):
    count = lax.axis_size(axis)
    initial, last = (max(0, -steps), min(count, count - steps))
    return lax.ppermute(value, axis, [(source, source + steps) for source in range(initial, last)])


def phase(numer, period):
    return (2.0 * math.pi / period) * (numer % period).astype(jnp.float32)


def transform_tables(shard_count, row_count):
    length = shard_count * row_count
    branch = jnp.arange(2, dtype=jnp.int32)
    shard = jnp.arange(shard_count, dtype=jnp.int32)
    row = jnp.arange(row_count, dtype=jnp.int32)
    theta = -phase(
        (2 * shard[:, None] * shard[None, :])[None] + branch[:, None, None] * shard[None, None, :],
        2 * shard_count,
    )
    stage_a = jnp.stack([jnp.cos(theta), jnp.sin(theta)], axis=1)
    phi = -phase(
        (2 * shard[:, None] * row[None, :])[None] + branch[:, None, None] * row[None, :][None],
        2 * length,
    )
    twiddle = (jnp.cos(phi), jnp.sin(phi))
    psi = -phase(row[:, None] * row[None, :], row_count)
    cos_b, sin_b = jnp.cos(psi), jnp.sin(psi)
    stage_b = jnp.stack(
        [jnp.stack([cos_b, sin_b], axis=1), jnp.stack([-sin_b, cos_b], axis=1)]
    )
    stage_b_inv = jnp.stack(
        [jnp.stack([cos_b, -sin_b], axis=1), jnp.stack([sin_b, cos_b], axis=1)]
    )
    stage_a_inv = stage_a * (0.5 / length)
    return stage_a, twiddle, stage_b, stage_b_inv, stage_a_inv


def complex_scale(value, cos_part, sin_part, axis):
    real_part = lax.index_in_dim(value, 0, axis, keepdims=False)
    imag_part = lax.index_in_dim(value, 1, axis, keepdims=False)
    return jnp.stack(
        [real_part * cos_part - imag_part * sin_part, real_part * sin_part + imag_part * cos_part],
        axis=axis,
    )


def to_columns(rows):
    shard_count = lax.axis_size("seq")
    batch, row_count, _ = rows.shape
    columns = lax.all_to_all(
        jnp.swapaxes(rows, 1, 2), "seq", split_axis=1, concat_axis=2, tiled=True
    )
    return columns.reshape(batch, columns.shape[1], shard_count, row_count)


def to_rows(columns):
    batch, chan_count, shard_count, row_count = columns.shape
    rows = lax.all_to_all(columns, "seq", split_axis=2, concat_axis=1, tiled=True)
    return jnp.swapaxes(rows.reshape(batch, shard_count * chan_count, row_count), 1, 2)


def forward_spectrum(columns, tables):
    stage_a, twiddle, stage_b, _, _ = tables
    spread = jnp.einsum("erkp,bcpm->bcerkm", stage_a, columns, precision=STAGE_A_PRECISION)
    spread = complex_scale(spread, twiddle[0], twiddle[1], 3)
    return jnp.einsum("bcerkm,rmsq->bceskq", spread, stage_b, precision=STAGE_B_PRECISION)


def inverse_spectrum(spectrum, tables):
    _, twiddle, _, stage_b_inv, stage_a_inv = tables
    spread = jnp.einsum("bceskq,sqrm->bcerkm", spectrum, stage_b_inv, precision=STAGE_B_PRECISION)
    spread = complex_scale(spread, twiddle[0], -twiddle[1], 3)
    return jnp.einsum("erkp,bcerkm->bcpm", stage_a_inv, spread, precision=STAGE_A_PRECISION)


def local(tokens, cotangent, in_weight, short_kernel, skip_gain, long_filter, out_weight):
    row_count = tokens.shape[0]
    tap_count = short_kernel.shape[0]
    shard_count = lax.axis_size("seq")
    tables = transform_tables(shard_count, row_count)
    filt_spec = forward_spectrum(to_columns(long_filter[None]), tables)
    both = lax.all_gather(
        jnp.concatenate([tokens, cotangent], axis=0), "panel", axis=1, tiled=True
    )
    full_tok, full_cot = both[:row_count], both[row_count:]
    projected = jnp.einsum(
        "td,jdc->jtc", full_tok, in_weight, preferred_element_type=jnp.float32
    ).astype(jnp.bfloat16)
    before = shifted(projected[:, row_count - (tap_count - 1) :, :], "seq", 1)
    extended = jnp.concatenate([before, projected], axis=1).astype(jnp.float32)
    filtered = short_kernel[0][:, None, :] * extended[:, tap_count - 1 :, :]
    for tap_index in range(1, tap_count):
        filtered = (
            filtered
            + short_kernel[tap_index][:, None, :]
            * extended[:, tap_count - 1 - tap_index : tap_count - 1 - tap_index + row_count, :]
        )
    gate_out, gate_in, value_path = (filtered[0], filtered[1], filtered[2])
    signal = value_path * gate_in
    grad_gated = lax.dot_general(
        full_cot, out_weight, (((1,), (1,)), ((), ())), preferred_element_type=jnp.float32
    )
    grad_state = grad_gated * gate_out
    spectra = forward_spectrum(to_columns(jnp.stack([signal, grad_state])), tables)
    filt_real, filt_imag = filt_spec[:, :, :, 0], filt_spec[:, :, :, 1]
    sig_real, sig_imag = spectra[0:1, :, :, 0], spectra[0:1, :, :, 1]
    grad_real, grad_imag = spectra[1:2, :, :, 0], spectra[1:2, :, :, 1]
    product = jnp.concatenate(
        [
            jnp.stack(
                [sig_real * filt_real - sig_imag * filt_imag, sig_real * filt_imag + sig_imag * filt_real],
                axis=3,
            ),
            jnp.stack(
                [grad_real * filt_real + grad_imag * filt_imag, grad_imag * filt_real - grad_real * filt_imag],
                axis=3,
            ),
        ]
    )
    convolved = to_rows(inverse_spectrum(product, tables))
    conv_state = convolved[0] + skip_gain[None, :] * signal
    grad_signal = convolved[1] + skip_gain[None, :] * grad_state
    gated_state = (conv_state * gate_out).astype(jnp.bfloat16)
    partial_value = jnp.dot(gated_state, out_weight, preferred_element_type=jnp.float32)
    block_out = lax.psum_scatter(
        partial_value.astype(jnp.bfloat16), "panel", scatter_dimension=1, tiled=True
    )
    grad_gate_out = grad_gated * conv_state
    grad_value = grad_signal * gate_in
    grad_gate_in = grad_signal * value_path
    upstream = jnp.stack([grad_gate_out, grad_gate_in, grad_value])
    after_rim = shifted(upstream[:, : tap_count - 1, :], "seq", -1)
    widened = jnp.concatenate([upstream, after_rim], axis=1)
    grad_projected = short_kernel[0][:, None, :] * widened[:, :row_count, :]
    for tap_index in range(1, tap_count):
        grad_projected = (
            grad_projected
            + short_kernel[tap_index][:, None, :] * widened[:, tap_index : tap_index + row_count, :]
        )
    grad_projected = grad_projected.astype(jnp.bfloat16)
    grad_partial = jnp.einsum(
        "jtc,jdc->td", grad_projected, in_weight, preferred_element_type=jnp.float32
    )
    token_grad = lax.psum_scatter(
        grad_partial.astype(jnp.bfloat16), "panel", scatter_dimension=1, tiled=True
    )
    return (block_out, token_grad)


def solution(mesh):
    placed = (
        P("seq", "panel"),
        P("seq", "panel"),
        P(None, None, "panel"),
        P(None, None, "panel"),
        P("panel"),
        P("seq", "panel"),
        P("panel", None),
    )
    return jax.shard_map(
        local,
        mesh=mesh,
        in_specs=placed,
        out_specs=(P("seq", "panel"), P("seq", "panel")),
        check_vma=False,
    )
```

```python
import math

import jax
import jax.numpy as jnp
from jax import lax
from jax.sharding import PartitionSpec as P

HIGHEST = lax.Precision.HIGHEST
STAGE_A_PRECISION = lax.Precision.HIGHEST
STAGE_B_PRECISION = lax.Precision.HIGH


def shifted(value, axis, steps):
    count = lax.axis_size(axis)
    initial, last = (max(0, -steps), min(count, count - steps))
    return lax.ppermute(value, axis, [(source, source + steps) for source in range(initial, last)])


def panel_gather(value):
    count = lax.axis_size("panel")
    me = lax.axis_index("panel")
    parts = [value] + [
        lax.ppermute(value, "panel", [(i, (i + k) % count) for i in range(count)])
        for k in range(count - 1, 0, -1)
    ]
    ordered = jnp.roll(jnp.stack(parts), me, axis=0)
    return jnp.concatenate([ordered[i] for i in range(count)], axis=-1)


def panel_reduce_scatter(value):
    count = lax.axis_size("panel")
    me = lax.axis_index("panel")
    rows, cols = value.shape
    blocks = jnp.roll(value.reshape(rows, count, cols // count), -me, axis=1)
    total = blocks[:, 0]
    for k in range(1, count):
        sent = blocks[:, k].astype(jnp.bfloat16)
        total = total + lax.ppermute(
            sent, "panel", [(i, (i + k) % count) for i in range(count)]
        ).astype(jnp.float32)
    return total.astype(jnp.bfloat16)


def phase(numer, period):
    return (2.0 * math.pi / period) * (numer % period).astype(jnp.float32)


def transform_tables(shard_count, row_count):
    length = shard_count * row_count
    branch = jnp.arange(2, dtype=jnp.int32)
    shard = jnp.arange(shard_count, dtype=jnp.int32)
    row = jnp.arange(row_count, dtype=jnp.int32)
    theta = -phase(
        (2 * shard[:, None] * shard[None, :])[None] + branch[:, None, None] * shard[None, None, :],
        2 * shard_count,
    )
    stage_a = jnp.stack([jnp.cos(theta), jnp.sin(theta)], axis=1)
    phi = -phase(
        (2 * shard[:, None] * row[None, :])[None] + branch[:, None, None] * row[None, :][None],
        2 * length,
    )
    twiddle = (jnp.cos(phi), jnp.sin(phi))
    psi = -phase(row[:, None] * row[None, :], row_count)
    cos_b, sin_b = jnp.cos(psi), jnp.sin(psi)
    stage_b = jnp.stack(
        [jnp.stack([cos_b, sin_b], axis=1), jnp.stack([-sin_b, cos_b], axis=1)]
    )
    stage_b_inv = jnp.stack(
        [jnp.stack([cos_b, -sin_b], axis=1), jnp.stack([sin_b, cos_b], axis=1)]
    )
    stage_a_inv = stage_a * (0.5 / length)
    return stage_a, twiddle, stage_b, stage_b_inv, stage_a_inv


def complex_scale(value, cos_part, sin_part, axis):
    real_part = lax.index_in_dim(value, 0, axis, keepdims=False)
    imag_part = lax.index_in_dim(value, 1, axis, keepdims=False)
    return jnp.stack(
        [real_part * cos_part - imag_part * sin_part, real_part * sin_part + imag_part * cos_part],
        axis=axis,
    )


def to_columns(rows):
    shard_count = lax.axis_size("seq")
    batch, row_count, _ = rows.shape
    columns = lax.all_to_all(
        jnp.swapaxes(rows, 1, 2), "seq", split_axis=1, concat_axis=2, tiled=True
    )
    return columns.reshape(batch, columns.shape[1], shard_count, row_count)


def to_rows(columns):
    batch, chan_count, shard_count, row_count = columns.shape
    rows = lax.all_to_all(columns, "seq", split_axis=2, concat_axis=1, tiled=True)
    return jnp.swapaxes(rows.reshape(batch, shard_count * chan_count, row_count), 1, 2)


def forward_spectrum(columns, tables):
    stage_a, twiddle, stage_b, _, _ = tables
    spread = jnp.einsum("erkp,bcpm->bcerkm", stage_a, columns, precision=STAGE_A_PRECISION)
    spread = complex_scale(spread, twiddle[0], twiddle[1], 3)
    return jnp.einsum("bcerkm,rmsq->bceskq", spread, stage_b, precision=STAGE_B_PRECISION)


def inverse_spectrum(spectrum, tables):
    _, twiddle, _, stage_b_inv, stage_a_inv = tables
    spread = jnp.einsum("bceskq,sqrm->bcerkm", spectrum, stage_b_inv, precision=STAGE_B_PRECISION)
    spread = complex_scale(spread, twiddle[0], -twiddle[1], 3)
    return jnp.einsum("erkp,bcerkm->bcpm", stage_a_inv, spread, precision=STAGE_A_PRECISION)


def local(tokens, cotangent, in_weight, short_kernel, skip_gain, long_filter, out_weight):
    row_count = tokens.shape[0]
    tap_count = short_kernel.shape[0]
    shard_count = lax.axis_size("seq")
    tables = transform_tables(shard_count, row_count)
    filt_spec = forward_spectrum(to_columns(long_filter[None]), tables)
    both = panel_gather(jnp.concatenate([tokens, cotangent], axis=0))
    full_tok, full_cot = both[:row_count], both[row_count:]
    projected = jnp.einsum(
        "td,jdc->jtc", full_tok, in_weight, preferred_element_type=jnp.float32
    ).astype(jnp.bfloat16)
    before = shifted(projected[:, row_count - (tap_count - 1) :, :], "seq", 1)
    extended = jnp.concatenate([before, projected], axis=1).astype(jnp.float32)
    filtered = short_kernel[0][:, None, :] * extended[:, tap_count - 1 :, :]
    for tap_index in range(1, tap_count):
        filtered = (
            filtered
            + short_kernel[tap_index][:, None, :]
            * extended[:, tap_count - 1 - tap_index : tap_count - 1 - tap_index + row_count, :]
        )
    gate_out, gate_in, value_path = (filtered[0], filtered[1], filtered[2])
    signal = value_path * gate_in
    grad_gated = lax.dot_general(
        full_cot, out_weight, (((1,), (1,)), ((), ())), preferred_element_type=jnp.float32
    )
    grad_state = grad_gated * gate_out
    spectra = forward_spectrum(to_columns(jnp.stack([signal, grad_state])), tables)
    filt_real, filt_imag = filt_spec[:, :, :, 0], filt_spec[:, :, :, 1]
    sig_real, sig_imag = spectra[0:1, :, :, 0], spectra[0:1, :, :, 1]
    grad_real, grad_imag = spectra[1:2, :, :, 0], spectra[1:2, :, :, 1]
    product = jnp.concatenate(
        [
            jnp.stack(
                [sig_real * filt_real - sig_imag * filt_imag, sig_real * filt_imag + sig_imag * filt_real],
                axis=3,
            ),
            jnp.stack(
                [grad_real * filt_real + grad_imag * filt_imag, grad_imag * filt_real - grad_real * filt_imag],
                axis=3,
            ),
        ]
    )
    convolved = to_rows(inverse_spectrum(product, tables))
    conv_state = convolved[0] + skip_gain[None, :] * signal
    grad_signal = convolved[1] + skip_gain[None, :] * grad_state
    gated_state = (conv_state * gate_out).astype(jnp.bfloat16)
    partial_value = jnp.dot(gated_state, out_weight, preferred_element_type=jnp.float32)
    block_out = panel_reduce_scatter(partial_value)
    grad_gate_out = grad_gated * conv_state
    grad_value = grad_signal * gate_in
    grad_gate_in = grad_signal * value_path
    upstream = jnp.stack([grad_gate_out, grad_gate_in, grad_value])
    after_rim = shifted(upstream[:, : tap_count - 1, :], "seq", -1)
    widened = jnp.concatenate([upstream, after_rim], axis=1)
    grad_projected = short_kernel[0][:, None, :] * widened[:, :row_count, :]
    for tap_index in range(1, tap_count):
        grad_projected = (
            grad_projected
            + short_kernel[tap_index][:, None, :] * widened[:, tap_index : tap_index + row_count, :]
        )
    grad_projected = grad_projected.astype(jnp.bfloat16)
    grad_partial = jnp.einsum(
        "jtc,jdc->td", grad_projected, in_weight, preferred_element_type=jnp.float32
    )
    token_grad = panel_reduce_scatter(grad_partial)
    return (block_out, token_grad)


def solution(mesh):
    placed = (
        P("seq", "panel"),
        P("seq", "panel"),
        P(None, None, "panel"),
        P(None, None, "panel"),
        P("panel"),
        P("seq", "panel"),
        P("panel", None),
    )
    return jax.shard_map(
        local,
        mesh=mesh,
        in_specs=placed,
        out_specs=(P("seq", "panel"), P("seq", "panel")),
        check_vma=False,
    )
```

```python
import math

import jax
import jax.numpy as jnp
from jax import lax
from jax.sharding import PartitionSpec as P

HIGHEST = lax.Precision.HIGHEST
STAGE_A_PRECISION = lax.Precision.HIGHEST
STAGE_B_PRECISION = lax.Precision.HIGH


def shifted(value, axis, steps):
    count = lax.axis_size(axis)
    initial, last = (max(0, -steps), min(count, count - steps))
    return lax.ppermute(value, axis, [(source, source + steps) for source in range(initial, last)])


def panel_parts(value):
    count = lax.axis_size("panel")
    me = lax.axis_index("panel")
    parts = [(value, me)]
    for k in range(1, count):
        moved = lax.ppermute(value, "panel", [(i, (i + k) % count) for i in range(count)])
        parts.append((moved, (me + count - k) % count))
    return parts


def panel_reduce_scatter(block_of):
    count = lax.axis_size("panel")
    me = lax.axis_index("panel")
    total = block_of(me)
    for k in range(1, count):
        sent = block_of((me + k) % count).astype(jnp.bfloat16)
        total = total + lax.ppermute(
            sent, "panel", [(i, (i + k) % count) for i in range(count)]
        ).astype(jnp.float32)
    return total.astype(jnp.bfloat16)


def phase(numer, period):
    return (2.0 * math.pi / period) * (numer % period).astype(jnp.float32)


def transform_tables(shard_count, row_count):
    length = shard_count * row_count
    branch = jnp.arange(2, dtype=jnp.int32)
    shard = jnp.arange(shard_count, dtype=jnp.int32)
    row = jnp.arange(row_count, dtype=jnp.int32)
    theta = -phase(
        (2 * shard[:, None] * shard[None, :])[None] + branch[:, None, None] * shard[None, None, :],
        2 * shard_count,
    )
    stage_a = jnp.stack([jnp.cos(theta), jnp.sin(theta)], axis=1)
    phi = -phase(
        (2 * shard[:, None] * row[None, :])[None] + branch[:, None, None] * row[None, :][None],
        2 * length,
    )
    twiddle = (jnp.cos(phi), jnp.sin(phi))
    psi = -phase(row[:, None] * row[None, :], row_count)
    cos_b, sin_b = jnp.cos(psi), jnp.sin(psi)
    stage_b = jnp.stack(
        [jnp.stack([cos_b, sin_b], axis=1), jnp.stack([-sin_b, cos_b], axis=1)]
    )
    stage_b_inv = jnp.stack(
        [jnp.stack([cos_b, -sin_b], axis=1), jnp.stack([sin_b, cos_b], axis=1)]
    )
    stage_a_inv = stage_a * (0.5 / length)
    return stage_a, twiddle, stage_b, stage_b_inv, stage_a_inv


def complex_scale(value, cos_part, sin_part, axis):
    real_part = lax.index_in_dim(value, 0, axis, keepdims=False)
    imag_part = lax.index_in_dim(value, 1, axis, keepdims=False)
    return jnp.stack(
        [real_part * cos_part - imag_part * sin_part, real_part * sin_part + imag_part * cos_part],
        axis=axis,
    )


def to_columns(rows):
    shard_count = lax.axis_size("seq")
    batch, row_count, _ = rows.shape
    columns = lax.all_to_all(
        jnp.swapaxes(rows, 1, 2), "seq", split_axis=1, concat_axis=2, tiled=True
    )
    return columns.reshape(batch, columns.shape[1], shard_count, row_count)


def to_rows(columns):
    batch, chan_count, shard_count, row_count = columns.shape
    rows = lax.all_to_all(columns, "seq", split_axis=2, concat_axis=1, tiled=True)
    return jnp.swapaxes(rows.reshape(batch, shard_count * chan_count, row_count), 1, 2)


def forward_spectrum(columns, tables):
    stage_a, twiddle, stage_b, _, _ = tables
    spread = jnp.einsum("erkp,bcpm->bcerkm", stage_a, columns, precision=STAGE_A_PRECISION)
    spread = complex_scale(spread, twiddle[0], twiddle[1], 3)
    return jnp.einsum("bcerkm,rmsq->bceskq", spread, stage_b, precision=STAGE_B_PRECISION)


def inverse_spectrum(spectrum, tables):
    _, twiddle, _, stage_b_inv, stage_a_inv = tables
    spread = jnp.einsum("bceskq,sqrm->bcerkm", spectrum, stage_b_inv, precision=STAGE_B_PRECISION)
    spread = complex_scale(spread, twiddle[0], -twiddle[1], 3)
    return jnp.einsum("erkp,bcerkm->bcpm", stage_a_inv, spread, precision=STAGE_A_PRECISION)


def local(tokens, cotangent, in_weight, short_kernel, skip_gain, long_filter, out_weight):
    row_count = tokens.shape[0]
    tap_count = short_kernel.shape[0]
    shard_count = lax.axis_size("seq")
    tables = transform_tables(shard_count, row_count)
    filt_spec = forward_spectrum(to_columns(long_filter[None]), tables)
    width = tokens.shape[1]
    parts = panel_parts(jnp.concatenate([tokens, cotangent], axis=0))
    projected = 0.0
    grad_gated = 0.0
    for part, source in parts:
        projected = projected + jnp.einsum(
            "td,jdc->jtc",
            part[:row_count],
            lax.dynamic_slice_in_dim(in_weight, source * width, width, axis=1),
            preferred_element_type=jnp.float32,
        )
        grad_gated = grad_gated + lax.dot_general(
            part[row_count:],
            lax.dynamic_slice_in_dim(out_weight, source * width, width, axis=1),
            (((1,), (1,)), ((), ())),
            preferred_element_type=jnp.float32,
        )
    projected = projected.astype(jnp.bfloat16)
    before = shifted(projected[:, row_count - (tap_count - 1) :, :], "seq", 1)
    extended = jnp.concatenate([before, projected], axis=1).astype(jnp.float32)
    filtered = short_kernel[0][:, None, :] * extended[:, tap_count - 1 :, :]
    for tap_index in range(1, tap_count):
        filtered = (
            filtered
            + short_kernel[tap_index][:, None, :]
            * extended[:, tap_count - 1 - tap_index : tap_count - 1 - tap_index + row_count, :]
        )
    gate_out, gate_in, value_path = (filtered[0], filtered[1], filtered[2])
    signal = value_path * gate_in
    grad_state = grad_gated * gate_out
    spectra = forward_spectrum(to_columns(jnp.stack([signal, grad_state])), tables)
    filt_real, filt_imag = filt_spec[:, :, :, 0], filt_spec[:, :, :, 1]
    sig_real, sig_imag = spectra[0:1, :, :, 0], spectra[0:1, :, :, 1]
    grad_real, grad_imag = spectra[1:2, :, :, 0], spectra[1:2, :, :, 1]
    product = jnp.concatenate(
        [
            jnp.stack(
                [sig_real * filt_real - sig_imag * filt_imag, sig_real * filt_imag + sig_imag * filt_real],
                axis=3,
            ),
            jnp.stack(
                [grad_real * filt_real + grad_imag * filt_imag, grad_imag * filt_real - grad_real * filt_imag],
                axis=3,
            ),
        ]
    )
    convolved = to_rows(inverse_spectrum(product, tables))
    conv_state = convolved[0] + skip_gain[None, :] * signal
    grad_signal = convolved[1] + skip_gain[None, :] * grad_state
    gated_state = (conv_state * gate_out).astype(jnp.bfloat16)
    block_out = panel_reduce_scatter(
        lambda dest: jnp.dot(
            gated_state,
            lax.dynamic_slice_in_dim(out_weight, dest * width, width, axis=1),
            preferred_element_type=jnp.float32,
        )
    )
    grad_gate_out = grad_gated * conv_state
    grad_value = grad_signal * gate_in
    grad_gate_in = grad_signal * value_path
    upstream = jnp.stack([grad_gate_out, grad_gate_in, grad_value])
    after_rim = shifted(upstream[:, : tap_count - 1, :], "seq", -1)
    widened = jnp.concatenate([upstream, after_rim], axis=1)
    grad_projected = short_kernel[0][:, None, :] * widened[:, :row_count, :]
    for tap_index in range(1, tap_count):
        grad_projected = (
            grad_projected
            + short_kernel[tap_index][:, None, :] * widened[:, tap_index : tap_index + row_count, :]
        )
    grad_projected = grad_projected.astype(jnp.bfloat16)
    token_grad = panel_reduce_scatter(
        lambda dest: jnp.einsum(
            "jtc,jdc->td",
            grad_projected,
            lax.dynamic_slice_in_dim(in_weight, dest * width, width, axis=1),
            preferred_element_type=jnp.float32,
        )
    )
    return (block_out, token_grad)


def solution(mesh):
    placed = (
        P("seq", "panel"),
        P("seq", "panel"),
        P(None, None, "panel"),
        P(None, None, "panel"),
        P("panel"),
        P("seq", "panel"),
        P("panel", None),
    )
    return jax.shard_map(
        local,
        mesh=mesh,
        in_specs=placed,
        out_specs=(P("seq", "panel"), P("seq", "panel")),
        check_vma=False,
    )
```

```python
import math

import jax
import jax.numpy as jnp
from jax import lax
from jax.sharding import PartitionSpec as P

HIGHEST = lax.Precision.HIGHEST
STAGE_A_PRECISION = lax.Precision.HIGHEST
STAGE_B_PRECISION = lax.Precision.HIGH
WIRE = jnp.float32


def shifted(value, axis, steps):
    count = lax.axis_size(axis)
    initial, last = (max(0, -steps), min(count, count - steps))
    return lax.ppermute(value, axis, [(source, source + steps) for source in range(initial, last)])


def panel_parts(value):
    count = lax.axis_size("panel")
    me = lax.axis_index("panel")
    parts = [(value, me)]
    for k in range(1, count):
        moved = lax.ppermute(value, "panel", [(i, (i + k) % count) for i in range(count)])
        parts.append((moved, (me + count - k) % count))
    return parts


def panel_reduce_scatter(block_of):
    count = lax.axis_size("panel")
    me = lax.axis_index("panel")
    total = block_of(me)
    for k in range(1, count):
        sent = block_of((me + k) % count).astype(jnp.bfloat16)
        total = total + lax.ppermute(
            sent, "panel", [(i, (i + k) % count) for i in range(count)]
        ).astype(jnp.float32)
    return total.astype(jnp.bfloat16)


def phase(numer, period):
    return (2.0 * math.pi / period) * (numer % period).astype(jnp.float32)


def transform_tables(shard_count, row_count):
    length = shard_count * row_count
    branch = jnp.arange(2, dtype=jnp.int32)
    shard = jnp.arange(shard_count, dtype=jnp.int32)
    row = jnp.arange(row_count, dtype=jnp.int32)
    theta = -phase(
        (2 * shard[:, None] * shard[None, :])[None] + branch[:, None, None] * shard[None, None, :],
        2 * shard_count,
    )
    stage_a = jnp.stack([jnp.cos(theta), jnp.sin(theta)], axis=1)
    phi = -phase(
        (2 * shard[:, None] * row[None, :])[None] + branch[:, None, None] * row[None, :][None],
        2 * length,
    )
    twiddle = (jnp.cos(phi), jnp.sin(phi))
    psi = -phase(row[:, None] * row[None, :], row_count)
    cos_b, sin_b = jnp.cos(psi), jnp.sin(psi)
    stage_b = jnp.stack(
        [jnp.stack([cos_b, sin_b], axis=1), jnp.stack([-sin_b, cos_b], axis=1)]
    )
    stage_b_inv = jnp.stack(
        [jnp.stack([cos_b, -sin_b], axis=1), jnp.stack([sin_b, cos_b], axis=1)]
    )
    stage_a_inv = stage_a * (0.5 / length)
    return stage_a, twiddle, stage_b, stage_b_inv, stage_a_inv


def complex_scale(value, cos_part, sin_part, axis):
    real_part = lax.index_in_dim(value, 0, axis, keepdims=False)
    imag_part = lax.index_in_dim(value, 1, axis, keepdims=False)
    return jnp.stack(
        [real_part * cos_part - imag_part * sin_part, real_part * sin_part + imag_part * cos_part],
        axis=axis,
    )


def to_columns(rows, wire=jnp.float32):
    shard_count = lax.axis_size("seq")
    batch, row_count, _ = rows.shape
    columns = lax.all_to_all(
        jnp.swapaxes(rows, 1, 2).astype(wire), "seq", split_axis=1, concat_axis=2, tiled=True
    ).astype(jnp.float32)
    return columns.reshape(batch, columns.shape[1], shard_count, row_count)


def to_rows(columns, wire=jnp.float32):
    batch, chan_count, shard_count, row_count = columns.shape
    rows = lax.all_to_all(
        columns.astype(wire), "seq", split_axis=2, concat_axis=1, tiled=True
    ).astype(jnp.float32)
    return jnp.swapaxes(rows.reshape(batch, shard_count * chan_count, row_count), 1, 2)


def forward_spectrum(columns, tables):
    stage_a, twiddle, stage_b, _, _ = tables
    spread = jnp.einsum("erkp,bcpm->bcerkm", stage_a, columns, precision=STAGE_A_PRECISION)
    spread = complex_scale(spread, twiddle[0], twiddle[1], 3)
    return jnp.einsum("bcerkm,rmsq->bceskq", spread, stage_b, precision=STAGE_B_PRECISION)


def inverse_spectrum(spectrum, tables):
    _, twiddle, _, stage_b_inv, stage_a_inv = tables
    spread = jnp.einsum("bceskq,sqrm->bcerkm", spectrum, stage_b_inv, precision=STAGE_B_PRECISION)
    spread = complex_scale(spread, twiddle[0], -twiddle[1], 3)
    return jnp.einsum("erkp,bcerkm->bcpm", stage_a_inv, spread, precision=STAGE_A_PRECISION)


def local(tokens, cotangent, in_weight, short_kernel, skip_gain, long_filter, out_weight):
    row_count = tokens.shape[0]
    tap_count = short_kernel.shape[0]
    shard_count = lax.axis_size("seq")
    tables = transform_tables(shard_count, row_count)
    filt_spec = forward_spectrum(to_columns(long_filter[None]), tables)
    width = tokens.shape[1]
    projected = 0.0
    for part, source in panel_parts(tokens):
        projected = projected + jnp.einsum(
            "td,jdc->jtc",
            part,
            lax.dynamic_slice_in_dim(in_weight, source * width, width, axis=1),
            preferred_element_type=jnp.float32,
        )
    grad_gated = 0.0
    for part, source in panel_parts(cotangent):
        grad_gated = grad_gated + lax.dot_general(
            part,
            lax.dynamic_slice_in_dim(out_weight, source * width, width, axis=1),
            (((1,), (1,)), ((), ())),
            preferred_element_type=jnp.float32,
        )
    projected = projected.astype(jnp.bfloat16)

    before = shifted(projected[:, row_count - (tap_count - 1) :, :], "seq", 1)
    extended = jnp.concatenate([before, projected], axis=1).astype(jnp.float32)
    filtered = short_kernel[0][:, None, :] * extended[:, tap_count - 1 :, :]
    for tap_index in range(1, tap_count):
        filtered = (
            filtered
            + short_kernel[tap_index][:, None, :]
            * extended[:, tap_count - 1 - tap_index : tap_count - 1 - tap_index + row_count, :]
        )
    gate_out, gate_in, value_path = (filtered[0], filtered[1], filtered[2])
    signal = value_path * gate_in
    grad_state = grad_gated * gate_out
    spectra = forward_spectrum(to_columns(jnp.stack([signal, grad_state]), WIRE), tables)
    filt_real, filt_imag = filt_spec[:, :, :, 0], filt_spec[:, :, :, 1]
    sig_real, sig_imag = spectra[0:1, :, :, 0], spectra[0:1, :, :, 1]
    grad_real, grad_imag = spectra[1:2, :, :, 0], spectra[1:2, :, :, 1]
    product = jnp.concatenate(
        [
            jnp.stack(
                [sig_real * filt_real - sig_imag * filt_imag, sig_real * filt_imag + sig_imag * filt_real],
                axis=3,
            ),
            jnp.stack(
                [grad_real * filt_real + grad_imag * filt_imag, grad_imag * filt_real - grad_real * filt_imag],
                axis=3,
            ),
        ]
    )
    convolved = to_rows(inverse_spectrum(product, tables), WIRE)
    conv_state = convolved[0] + skip_gain[None, :] * signal
    grad_signal = convolved[1] + skip_gain[None, :] * grad_state
    gated_state = (conv_state * gate_out).astype(jnp.bfloat16)
    block_out = panel_reduce_scatter(
        lambda dest: jnp.dot(
            gated_state,
            lax.dynamic_slice_in_dim(out_weight, dest * width, width, axis=1),
            preferred_element_type=jnp.float32,
        )
    )
    grad_gate_out = grad_gated * conv_state
    grad_value = grad_signal * gate_in
    grad_gate_in = grad_signal * value_path
    upstream = jnp.stack([grad_gate_out, grad_gate_in, grad_value])
    after_rim = shifted(upstream[:, : tap_count - 1, :], "seq", -1)
    widened = jnp.concatenate([upstream, after_rim], axis=1)
    grad_projected = short_kernel[0][:, None, :] * widened[:, :row_count, :]
    for tap_index in range(1, tap_count):
        grad_projected = (
            grad_projected
            + short_kernel[tap_index][:, None, :] * widened[:, tap_index : tap_index + row_count, :]
        )
    grad_projected = grad_projected.astype(jnp.bfloat16)
    token_grad = panel_reduce_scatter(
        lambda dest: jnp.einsum(
            "jtc,jdc->td",
            grad_projected,
            lax.dynamic_slice_in_dim(in_weight, dest * width, width, axis=1),
            preferred_element_type=jnp.float32,
        )
    )
    return (block_out, token_grad)


def solution(mesh):
    placed = (
        P("seq", "panel"),
        P("seq", "panel"),
        P(None, None, "panel"),
        P(None, None, "panel"),
        P("panel"),
        P("seq", "panel"),
        P("panel", None),
    )
    return jax.shard_map(
        local,
        mesh=mesh,
        in_specs=placed,
        out_specs=(P("seq", "panel"), P("seq", "panel")),
        check_vma=False,
    )
```

```python
import math

import jax
import jax.numpy as jnp
from jax import lax
from jax.sharding import PartitionSpec as P

HIGHEST = lax.Precision.HIGHEST
STAGE_A_PRECISION = lax.Precision.HIGHEST
STAGE_B_PRECISION = lax.Precision.HIGH
WIRE = jnp.bfloat16


def shifted(value, axis, steps):
    count = lax.axis_size(axis)
    initial, last = (max(0, -steps), min(count, count - steps))
    return lax.ppermute(value, axis, [(source, source + steps) for source in range(initial, last)])


def panel_parts(value):
    count = lax.axis_size("panel")
    me = lax.axis_index("panel")
    parts = [(value, me)]
    for k in range(1, count):
        moved = lax.ppermute(value, "panel", [(i, (i + k) % count) for i in range(count)])
        parts.append((moved, (me + count - k) % count))
    return parts


def panel_reduce_scatter(block_of):
    count = lax.axis_size("panel")
    me = lax.axis_index("panel")
    total = block_of(me)
    for k in range(1, count):
        sent = block_of((me + k) % count).astype(jnp.bfloat16)
        total = total + lax.ppermute(
            sent, "panel", [(i, (i + k) % count) for i in range(count)]
        ).astype(jnp.float32)
    return total.astype(jnp.bfloat16)


def phase(numer, period):
    return (2.0 * math.pi / period) * (numer % period).astype(jnp.float32)


def transform_tables(shard_count, row_count):
    length = shard_count * row_count
    branch = jnp.arange(2, dtype=jnp.int32)
    shard = jnp.arange(shard_count, dtype=jnp.int32)
    row = jnp.arange(row_count, dtype=jnp.int32)
    theta = -phase(
        (2 * shard[:, None] * shard[None, :])[None] + branch[:, None, None] * shard[None, None, :],
        2 * shard_count,
    )
    stage_a = jnp.stack([jnp.cos(theta), jnp.sin(theta)], axis=1)
    phi = -phase(
        (2 * shard[:, None] * row[None, :])[None] + branch[:, None, None] * row[None, :][None],
        2 * length,
    )
    twiddle = (jnp.cos(phi), jnp.sin(phi))
    psi = -phase(row[:, None] * row[None, :], row_count)
    cos_b, sin_b = jnp.cos(psi), jnp.sin(psi)
    stage_b = jnp.stack(
        [jnp.stack([cos_b, sin_b], axis=1), jnp.stack([-sin_b, cos_b], axis=1)]
    )
    stage_b_inv = jnp.stack(
        [jnp.stack([cos_b, -sin_b], axis=1), jnp.stack([sin_b, cos_b], axis=1)]
    )
    stage_a_inv = stage_a * (0.5 / length)
    return stage_a, twiddle, stage_b, stage_b_inv, stage_a_inv


def complex_scale(value, cos_part, sin_part, axis):
    real_part = lax.index_in_dim(value, 0, axis, keepdims=False)
    imag_part = lax.index_in_dim(value, 1, axis, keepdims=False)
    return jnp.stack(
        [real_part * cos_part - imag_part * sin_part, real_part * sin_part + imag_part * cos_part],
        axis=axis,
    )


def to_columns(rows, wire=jnp.float32):
    shard_count = lax.axis_size("seq")
    batch, row_count, _ = rows.shape
    columns = lax.all_to_all(
        jnp.swapaxes(rows, 1, 2).astype(wire), "seq", split_axis=1, concat_axis=2, tiled=True
    ).astype(jnp.float32)
    return columns.reshape(batch, columns.shape[1], shard_count, row_count)


def to_rows(columns, wire=jnp.float32):
    batch, chan_count, shard_count, row_count = columns.shape
    rows = lax.all_to_all(
        columns.astype(wire), "seq", split_axis=2, concat_axis=1, tiled=True
    ).astype(jnp.float32)
    return jnp.swapaxes(rows.reshape(batch, shard_count * chan_count, row_count), 1, 2)


def forward_spectrum(columns, tables):
    stage_a, twiddle, stage_b, _, _ = tables
    spread = jnp.einsum("erkp,bcpm->bcerkm", stage_a, columns, precision=STAGE_A_PRECISION)
    spread = complex_scale(spread, twiddle[0], twiddle[1], 3)
    return jnp.einsum("bcerkm,rmsq->bceskq", spread, stage_b, precision=STAGE_B_PRECISION)


def inverse_spectrum(spectrum, tables):
    _, twiddle, _, stage_b_inv, stage_a_inv = tables
    spread = jnp.einsum("bceskq,sqrm->bcerkm", spectrum, stage_b_inv, precision=STAGE_B_PRECISION)
    spread = complex_scale(spread, twiddle[0], -twiddle[1], 3)
    return jnp.einsum("erkp,bcerkm->bcpm", stage_a_inv, spread, precision=STAGE_A_PRECISION)


def local(tokens, cotangent, in_weight, short_kernel, skip_gain, long_filter, out_weight):
    row_count = tokens.shape[0]
    tap_count = short_kernel.shape[0]
    shard_count = lax.axis_size("seq")
    tables = transform_tables(shard_count, row_count)
    filt_spec = forward_spectrum(to_columns(long_filter[None]), tables)
    width = tokens.shape[1]
    projected = 0.0
    for part, source in panel_parts(tokens):
        projected = projected + jnp.einsum(
            "td,jdc->jtc",
            part,
            lax.dynamic_slice_in_dim(in_weight, source * width, width, axis=1),
            preferred_element_type=jnp.float32,
        )
    grad_gated = 0.0
    for part, source in panel_parts(cotangent):
        grad_gated = grad_gated + lax.dot_general(
            part,
            lax.dynamic_slice_in_dim(out_weight, source * width, width, axis=1),
            (((1,), (1,)), ((), ())),
            preferred_element_type=jnp.float32,
        )
    projected = projected.astype(jnp.bfloat16)

    before = shifted(projected[:, row_count - (tap_count - 1) :, :], "seq", 1)
    extended = jnp.concatenate([before, projected], axis=1).astype(jnp.float32)
    filtered = short_kernel[0][:, None, :] * extended[:, tap_count - 1 :, :]
    for tap_index in range(1, tap_count):
        filtered = (
            filtered
            + short_kernel[tap_index][:, None, :]
            * extended[:, tap_count - 1 - tap_index : tap_count - 1 - tap_index + row_count, :]
        )
    gate_out, gate_in, value_path = (filtered[0], filtered[1], filtered[2])
    signal = value_path * gate_in
    grad_state = grad_gated * gate_out
    spectra = forward_spectrum(to_columns(jnp.stack([signal, grad_state]), WIRE), tables)
    filt_real, filt_imag = filt_spec[:, :, :, 0], filt_spec[:, :, :, 1]
    sig_real, sig_imag = spectra[0:1, :, :, 0], spectra[0:1, :, :, 1]
    grad_real, grad_imag = spectra[1:2, :, :, 0], spectra[1:2, :, :, 1]
    product = jnp.concatenate(
        [
            jnp.stack(
                [sig_real * filt_real - sig_imag * filt_imag, sig_real * filt_imag + sig_imag * filt_real],
                axis=3,
            ),
            jnp.stack(
                [grad_real * filt_real + grad_imag * filt_imag, grad_imag * filt_real - grad_real * filt_imag],
                axis=3,
            ),
        ]
    )
    convolved = to_rows(inverse_spectrum(product, tables), WIRE)
    conv_state = convolved[0] + skip_gain[None, :] * signal
    grad_signal = convolved[1] + skip_gain[None, :] * grad_state
    gated_state = (conv_state * gate_out).astype(jnp.bfloat16)
    block_out = panel_reduce_scatter(
        lambda dest: jnp.dot(
            gated_state,
            lax.dynamic_slice_in_dim(out_weight, dest * width, width, axis=1),
            preferred_element_type=jnp.float32,
        )
    )
    grad_gate_out = grad_gated * conv_state
    grad_value = grad_signal * gate_in
    grad_gate_in = grad_signal * value_path
    upstream = jnp.stack([grad_gate_out, grad_gate_in, grad_value])
    after_rim = shifted(upstream[:, : tap_count - 1, :], "seq", -1)
    widened = jnp.concatenate([upstream, after_rim], axis=1)
    grad_projected = short_kernel[0][:, None, :] * widened[:, :row_count, :]
    for tap_index in range(1, tap_count):
        grad_projected = (
            grad_projected
            + short_kernel[tap_index][:, None, :] * widened[:, tap_index : tap_index + row_count, :]
        )
    grad_projected = grad_projected.astype(jnp.bfloat16)
    token_grad = panel_reduce_scatter(
        lambda dest: jnp.einsum(
            "jtc,jdc->td",
            grad_projected,
            lax.dynamic_slice_in_dim(in_weight, dest * width, width, axis=1),
            preferred_element_type=jnp.float32,
        )
    )
    return (block_out, token_grad)


def solution(mesh):
    placed = (
        P("seq", "panel"),
        P("seq", "panel"),
        P(None, None, "panel"),
        P(None, None, "panel"),
        P("panel"),
        P("seq", "panel"),
        P("panel", None),
    )
    return jax.shard_map(
        local,
        mesh=mesh,
        in_specs=placed,
        out_specs=(P("seq", "panel"), P("seq", "panel")),
        check_vma=False,
    )
```

```python
import math

import jax
import jax.numpy as jnp
from jax import lax
from jax.sharding import PartitionSpec as P

HIGHEST = lax.Precision.HIGHEST
STAGE_A_PRECISION = lax.Precision.HIGHEST
STAGE_B_PRECISION = lax.Precision.HIGH
WIRE = jnp.bfloat16


def shifted(value, axis, steps):
    count = lax.axis_size(axis)
    initial, last = (max(0, -steps), min(count, count - steps))
    return lax.ppermute(value, axis, [(source, source + steps) for source in range(initial, last)])


def panel_shift(value, steps):
    count = lax.axis_size("panel")
    return lax.ppermute(value, "panel", [(i, (i + steps) % count) for i in range(count)])


def panel_parts(value):
    count = lax.axis_size("panel")
    me = lax.axis_index("panel")
    parts = [(value, me)]
    left, right = value, value
    for distance in range(1, (count + 1) // 2):
        left, right = panel_shift(left, 1), panel_shift(right, -1)
        parts.append((left, (me + count - distance) % count))
        parts.append((right, (me + distance) % count))
    if count % 2 == 0 and count > 1:
        half = value.shape[0] // 2
        far = jnp.concatenate(
            [panel_shift(left[:half], 1), panel_shift(right[half:], -1)], axis=0
        )
        parts.append((far, (me + count // 2) % count))
    return parts


def panel_reduce_scatter(block_of):
    count = lax.axis_size("panel")
    me = lax.axis_index("panel")
    total = block_of(me)
    for k in range(1, count):
        sent = block_of((me + k) % count).astype(jnp.bfloat16)
        total = total + lax.ppermute(
            sent, "panel", [(i, (i + k) % count) for i in range(count)]
        ).astype(jnp.float32)
    return total.astype(jnp.bfloat16)


def phase(numer, period):
    return (2.0 * math.pi / period) * (numer % period).astype(jnp.float32)


def transform_tables(shard_count, row_count):
    length = shard_count * row_count
    branch = jnp.arange(2, dtype=jnp.int32)
    shard = jnp.arange(shard_count, dtype=jnp.int32)
    row = jnp.arange(row_count, dtype=jnp.int32)
    theta = -phase(
        (2 * shard[:, None] * shard[None, :])[None] + branch[:, None, None] * shard[None, None, :],
        2 * shard_count,
    )
    stage_a = jnp.stack([jnp.cos(theta), jnp.sin(theta)], axis=1)
    phi = -phase(
        (2 * shard[:, None] * row[None, :])[None] + branch[:, None, None] * row[None, :][None],
        2 * length,
    )
    twiddle = (jnp.cos(phi), jnp.sin(phi))
    psi = -phase(row[:, None] * row[None, :], row_count)
    cos_b, sin_b = jnp.cos(psi), jnp.sin(psi)
    stage_b = jnp.stack(
        [jnp.stack([cos_b, sin_b], axis=1), jnp.stack([-sin_b, cos_b], axis=1)]
    )
    stage_b_inv = jnp.stack(
        [jnp.stack([cos_b, -sin_b], axis=1), jnp.stack([sin_b, cos_b], axis=1)]
    )
    stage_a_inv = stage_a * (0.5 / length)
    return stage_a, twiddle, stage_b, stage_b_inv, stage_a_inv


def complex_scale(value, cos_part, sin_part, axis):
    real_part = lax.index_in_dim(value, 0, axis, keepdims=False)
    imag_part = lax.index_in_dim(value, 1, axis, keepdims=False)
    return jnp.stack(
        [real_part * cos_part - imag_part * sin_part, real_part * sin_part + imag_part * cos_part],
        axis=axis,
    )


def to_columns(rows, wire=jnp.float32):
    shard_count = lax.axis_size("seq")
    batch, row_count, _ = rows.shape
    columns = lax.all_to_all(
        jnp.swapaxes(rows, 1, 2).astype(wire), "seq", split_axis=1, concat_axis=2, tiled=True
    ).astype(jnp.float32)
    return columns.reshape(batch, columns.shape[1], shard_count, row_count)


def to_rows(columns, wire=jnp.float32):
    batch, chan_count, shard_count, row_count = columns.shape
    rows = lax.all_to_all(
        columns.astype(wire), "seq", split_axis=2, concat_axis=1, tiled=True
    ).astype(jnp.float32)
    return jnp.swapaxes(rows.reshape(batch, shard_count * chan_count, row_count), 1, 2)


def forward_spectrum(columns, tables):
    stage_a, twiddle, stage_b, _, _ = tables
    spread = jnp.einsum("erkp,bcpm->bcerkm", stage_a, columns, precision=STAGE_A_PRECISION)
    spread = complex_scale(spread, twiddle[0], twiddle[1], 3)
    return jnp.einsum("bcerkm,rmsq->bceskq", spread, stage_b, precision=STAGE_B_PRECISION)


def inverse_spectrum(spectrum, tables):
    _, twiddle, _, stage_b_inv, stage_a_inv = tables
    spread = jnp.einsum("bceskq,sqrm->bcerkm", spectrum, stage_b_inv, precision=STAGE_B_PRECISION)
    spread = complex_scale(spread, twiddle[0], -twiddle[1], 3)
    return jnp.einsum("erkp,bcerkm->bcpm", stage_a_inv, spread, precision=STAGE_A_PRECISION)


def local(tokens, cotangent, in_weight, short_kernel, skip_gain, long_filter, out_weight):
    row_count = tokens.shape[0]
    tap_count = short_kernel.shape[0]
    shard_count = lax.axis_size("seq")
    tables = transform_tables(shard_count, row_count)
    filt_spec = forward_spectrum(to_columns(long_filter[None]), tables)
    width = tokens.shape[1]
    projected = 0.0
    for part, source in panel_parts(tokens):
        projected = projected + jnp.einsum(
            "td,jdc->jtc",
            part,
            lax.dynamic_slice_in_dim(in_weight, source * width, width, axis=1),
            preferred_element_type=jnp.float32,
        )
    grad_gated = 0.0
    for part, source in panel_parts(cotangent):
        grad_gated = grad_gated + lax.dot_general(
            part,
            lax.dynamic_slice_in_dim(out_weight, source * width, width, axis=1),
            (((1,), (1,)), ((), ())),
            preferred_element_type=jnp.float32,
        )
    projected = projected.astype(jnp.bfloat16)

    before = shifted(projected[:, row_count - (tap_count - 1) :, :], "seq", 1)
    extended = jnp.concatenate([before, projected], axis=1).astype(jnp.float32)
    filtered = short_kernel[0][:, None, :] * extended[:, tap_count - 1 :, :]
    for tap_index in range(1, tap_count):
        filtered = (
            filtered
            + short_kernel[tap_index][:, None, :]
            * extended[:, tap_count - 1 - tap_index : tap_count - 1 - tap_index + row_count, :]
        )
    gate_out, gate_in, value_path = (filtered[0], filtered[1], filtered[2])
    signal = value_path * gate_in
    grad_state = grad_gated * gate_out
    spectra = forward_spectrum(to_columns(jnp.stack([signal, grad_state]), WIRE), tables)
    filt_real, filt_imag = filt_spec[:, :, :, 0], filt_spec[:, :, :, 1]
    sig_real, sig_imag = spectra[0:1, :, :, 0], spectra[0:1, :, :, 1]
    grad_real, grad_imag = spectra[1:2, :, :, 0], spectra[1:2, :, :, 1]
    product = jnp.concatenate(
        [
            jnp.stack(
                [sig_real * filt_real - sig_imag * filt_imag, sig_real * filt_imag + sig_imag * filt_real],
                axis=3,
            ),
            jnp.stack(
                [grad_real * filt_real + grad_imag * filt_imag, grad_imag * filt_real - grad_real * filt_imag],
                axis=3,
            ),
        ]
    )
    convolved = to_rows(inverse_spectrum(product, tables), WIRE)
    conv_state = convolved[0] + skip_gain[None, :] * signal
    grad_signal = convolved[1] + skip_gain[None, :] * grad_state
    gated_state = (conv_state * gate_out).astype(jnp.bfloat16)
    block_out = panel_reduce_scatter(
        lambda dest: jnp.dot(
            gated_state,
            lax.dynamic_slice_in_dim(out_weight, dest * width, width, axis=1),
            preferred_element_type=jnp.float32,
        )
    )
    grad_gate_out = grad_gated * conv_state
    grad_value = grad_signal * gate_in
    grad_gate_in = grad_signal * value_path
    upstream = jnp.stack([grad_gate_out, grad_gate_in, grad_value])
    after_rim = shifted(upstream[:, : tap_count - 1, :], "seq", -1)
    widened = jnp.concatenate([upstream, after_rim], axis=1)
    grad_projected = short_kernel[0][:, None, :] * widened[:, :row_count, :]
    for tap_index in range(1, tap_count):
        grad_projected = (
            grad_projected
            + short_kernel[tap_index][:, None, :] * widened[:, tap_index : tap_index + row_count, :]
        )
    grad_projected = grad_projected.astype(jnp.bfloat16)
    token_grad = panel_reduce_scatter(
        lambda dest: jnp.einsum(
            "jtc,jdc->td",
            grad_projected,
            lax.dynamic_slice_in_dim(in_weight, dest * width, width, axis=1),
            preferred_element_type=jnp.float32,
        )
    )
    return (block_out, token_grad)


def solution(mesh):
    placed = (
        P("seq", "panel"),
        P("seq", "panel"),
        P(None, None, "panel"),
        P(None, None, "panel"),
        P("panel"),
        P("seq", "panel"),
        P("panel", None),
    )
    return jax.shard_map(
        local,
        mesh=mesh,
        in_specs=placed,
        out_specs=(P("seq", "panel"), P("seq", "panel")),
        check_vma=False,
    )
```

```python
import math

import jax
import jax.numpy as jnp
from jax import lax
from jax.sharding import PartitionSpec as P

HIGHEST = lax.Precision.HIGHEST
STAGE_A_PRECISION = lax.Precision.HIGHEST
STAGE_B_PRECISION = lax.Precision.HIGH
WIRE = jnp.bfloat16


def shifted(value, axis, steps):
    count = lax.axis_size(axis)
    initial, last = (max(0, -steps), min(count, count - steps))
    return lax.ppermute(value, axis, [(source, source + steps) for source in range(initial, last)])


def panel_parts(value):
    count = lax.axis_size("panel")
    me = lax.axis_index("panel")
    parts = [(value, me)]
    for k in range(1, count):
        moved = lax.ppermute(value, "panel", [(i, (i + k) % count) for i in range(count)])
        parts.append((moved, (me + count - k) % count))
    return parts


def panel_reduce_scatter(block_of):
    count = lax.axis_size("panel")
    me = lax.axis_index("panel")
    total = block_of(me)
    for k in range(1, count):
        sent = block_of((me + k) % count).astype(jnp.bfloat16)
        total = total + lax.ppermute(
            sent, "panel", [(i, (i + k) % count) for i in range(count)]
        ).astype(jnp.float32)
    return total.astype(jnp.bfloat16)


def phase(numer, period):
    return (2.0 * math.pi / period) * (numer % period).astype(jnp.float32)


def transform_tables(shard_count, row_count):
    length = shard_count * row_count
    branch = jnp.arange(2, dtype=jnp.int32)
    shard = jnp.arange(shard_count, dtype=jnp.int32)
    row = jnp.arange(row_count, dtype=jnp.int32)
    theta = -phase(
        (2 * shard[:, None] * shard[None, :])[None] + branch[:, None, None] * shard[None, None, :],
        2 * shard_count,
    )
    stage_a = jnp.stack([jnp.cos(theta), jnp.sin(theta)], axis=1)
    phi = -phase(
        (2 * shard[:, None] * row[None, :])[None] + branch[:, None, None] * row[None, :][None],
        2 * length,
    )
    twiddle = (jnp.cos(phi), jnp.sin(phi))
    psi = -phase(row[:, None] * row[None, :], row_count)
    cos_b, sin_b = jnp.cos(psi), jnp.sin(psi)
    stage_b = jnp.stack(
        [jnp.stack([cos_b, sin_b], axis=1), jnp.stack([-sin_b, cos_b], axis=1)]
    )
    stage_b_inv = jnp.stack(
        [jnp.stack([cos_b, -sin_b], axis=1), jnp.stack([sin_b, cos_b], axis=1)]
    )
    stage_a_inv = stage_a * (0.5 / length)
    return stage_a, twiddle, stage_b, stage_b_inv, stage_a_inv


def complex_scale(value, cos_part, sin_part, axis):
    real_part = lax.index_in_dim(value, 0, axis, keepdims=False)
    imag_part = lax.index_in_dim(value, 1, axis, keepdims=False)
    return jnp.stack(
        [real_part * cos_part - imag_part * sin_part, real_part * sin_part + imag_part * cos_part],
        axis=axis,
    )


def to_columns(rows, wire=jnp.float32):
    shard_count = lax.axis_size("seq")
    batch, row_count, _ = rows.shape
    columns = lax.all_to_all(
        jnp.swapaxes(rows, 1, 2).astype(wire), "seq", split_axis=1, concat_axis=2, tiled=True
    ).astype(jnp.float32)
    return columns.reshape(batch, columns.shape[1], shard_count, row_count)


def to_rows(columns, wire=jnp.float32):
    batch, chan_count, shard_count, row_count = columns.shape
    rows = lax.all_to_all(
        columns.astype(wire), "seq", split_axis=2, concat_axis=1, tiled=True
    ).astype(jnp.float32)
    return jnp.swapaxes(rows.reshape(batch, shard_count * chan_count, row_count), 1, 2)


def forward_spectrum(columns, tables):
    stage_a, twiddle, stage_b, _, _ = tables
    spread = jnp.einsum("erkp,bcpm->bcerkm", stage_a, columns, precision=STAGE_A_PRECISION)
    spread = complex_scale(spread, twiddle[0], twiddle[1], 3)
    return jnp.einsum("bcerkm,rmsq->bceskq", spread, stage_b, precision=STAGE_B_PRECISION)


def inverse_spectrum(spectrum, tables):
    _, twiddle, _, stage_b_inv, stage_a_inv = tables
    spread = jnp.einsum("bceskq,sqrm->bcerkm", spectrum, stage_b_inv, precision=STAGE_B_PRECISION)
    spread = complex_scale(spread, twiddle[0], -twiddle[1], 3)
    return jnp.einsum("erkp,bcerkm->bcpm", stage_a_inv, spread, precision=STAGE_A_PRECISION)


def local(tokens, cotangent, in_weight, short_kernel, skip_gain, long_filter, out_weight):
    row_count = tokens.shape[0]
    tap_count = short_kernel.shape[0]
    shard_count = lax.axis_size("seq")
    tables = transform_tables(shard_count, row_count)
    filt_spec = forward_spectrum(to_columns(long_filter[None]), tables)
    width = tokens.shape[1]
    projected = 0.0
    for part, source in panel_parts(tokens):
        projected = projected + jnp.einsum(
            "td,jdc->jtc",
            part,
            lax.dynamic_slice_in_dim(in_weight, source * width, width, axis=1),
            preferred_element_type=jnp.float32,
        )
    grad_gated = 0.0
    for part, source in panel_parts(cotangent):
        grad_gated = grad_gated + lax.dot_general(
            part,
            lax.dynamic_slice_in_dim(out_weight, source * width, width, axis=1),
            (((1,), (1,)), ((), ())),
            preferred_element_type=jnp.float32,
        )
    projected = projected.astype(jnp.bfloat16)

    before = shifted(projected[:, row_count - (tap_count - 1) :, :], "seq", 1)
    extended = jnp.concatenate([before, projected], axis=1).astype(jnp.float32)
    filtered = short_kernel[0][:, None, :] * extended[:, tap_count - 1 :, :]
    for tap_index in range(1, tap_count):
        filtered = (
            filtered
            + short_kernel[tap_index][:, None, :]
            * extended[:, tap_count - 1 - tap_index : tap_count - 1 - tap_index + row_count, :]
        )
    gate_out, gate_in, value_path = (filtered[0], filtered[1], filtered[2])
    signal = value_path * gate_in
    grad_state = grad_gated * gate_out
    spectra = forward_spectrum(to_columns(jnp.stack([signal, grad_state]), WIRE), tables)
    filt_real, filt_imag = filt_spec[:, :, :, 0], filt_spec[:, :, :, 1]
    sig_real, sig_imag = spectra[0:1, :, :, 0], spectra[0:1, :, :, 1]
    grad_real, grad_imag = spectra[1:2, :, :, 0], spectra[1:2, :, :, 1]
    product = jnp.concatenate(
        [
            jnp.stack(
                [sig_real * filt_real - sig_imag * filt_imag, sig_real * filt_imag + sig_imag * filt_real],
                axis=3,
            ),
            jnp.stack(
                [grad_real * filt_real + grad_imag * filt_imag, grad_imag * filt_real - grad_real * filt_imag],
                axis=3,
            ),
        ]
    )
    convolved = to_rows(inverse_spectrum(product, tables), WIRE)
    conv_state = convolved[0] + skip_gain[None, :] * signal
    grad_signal = convolved[1] + skip_gain[None, :] * grad_state
    gated_state = (conv_state * gate_out).astype(jnp.bfloat16)
    grad_gate_out = grad_gated * conv_state
    grad_value = grad_signal * gate_in
    grad_gate_in = grad_signal * value_path
    upstream = jnp.stack([grad_gate_out, grad_gate_in, grad_value])
    after_rim = shifted(upstream[:, : tap_count - 1, :], "seq", -1)
    widened = jnp.concatenate([upstream, after_rim], axis=1)
    grad_projected = short_kernel[0][:, None, :] * widened[:, :row_count, :]
    for tap_index in range(1, tap_count):
        grad_projected = (
            grad_projected
            + short_kernel[tap_index][:, None, :] * widened[:, tap_index : tap_index + row_count, :]
        )
    grad_projected = grad_projected.astype(jnp.bfloat16)
    outputs = panel_reduce_scatter(
        lambda dest: jnp.stack(
            [
                jnp.dot(
                    gated_state,
                    lax.dynamic_slice_in_dim(out_weight, dest * width, width, axis=1),
                    preferred_element_type=jnp.float32,
                ),
                jnp.einsum(
                    "jtc,jdc->td",
                    grad_projected,
                    lax.dynamic_slice_in_dim(in_weight, dest * width, width, axis=1),
                    preferred_element_type=jnp.float32,
                ),
            ]
        )
    )
    return (outputs[0], outputs[1])


def solution(mesh):
    placed = (
        P("seq", "panel"),
        P("seq", "panel"),
        P(None, None, "panel"),
        P(None, None, "panel"),
        P("panel"),
        P("seq", "panel"),
        P("panel", None),
    )
    return jax.shard_map(
        local,
        mesh=mesh,
        in_specs=placed,
        out_specs=(P("seq", "panel"), P("seq", "panel")),
        check_vma=False,
    )
```

```python
import math

import jax
import jax.numpy as jnp
from jax import lax
from jax.sharding import PartitionSpec as P


STAGE_A_PRECISION = lax.Precision.HIGHEST
STAGE_B_PRECISION = lax.Precision.HIGH
WIRE = jnp.bfloat16


def shifted(value, axis, steps):
    count = lax.axis_size(axis)
    initial, last = (max(0, -steps), min(count, count - steps))
    return lax.ppermute(value, axis, [(source, source + steps) for source in range(initial, last)])


def panel_parts(value):
    count = lax.axis_size("panel")
    me = lax.axis_index("panel")
    parts = [(value, me)]
    for k in range(1, count):
        moved = lax.ppermute(value, "panel", [(i, (i + k) % count) for i in range(count)])
        parts.append((moved, (me + count - k) % count))
    return parts


def panel_reduce_scatter(block_of):
    count = lax.axis_size("panel")
    me = lax.axis_index("panel")
    total = block_of(me)
    for k in range(1, count):
        sent = block_of((me + k) % count).astype(jnp.bfloat16)
        total = total + lax.ppermute(
            sent, "panel", [(i, (i + k) % count) for i in range(count)]
        ).astype(jnp.float32)
    return total.astype(jnp.bfloat16)


def phase(numer, period):
    return (2.0 * math.pi / period) * (numer % period).astype(jnp.float32)


def transform_tables(shard_count, row_count):
    length = shard_count * row_count
    branch = jnp.arange(2, dtype=jnp.int32)
    shard = jnp.arange(shard_count, dtype=jnp.int32)
    row = jnp.arange(row_count, dtype=jnp.int32)
    theta = -phase(
        (2 * shard[:, None] * shard[None, :])[None] + branch[:, None, None] * shard[None, None, :],
        2 * shard_count,
    )
    stage_a = jnp.stack([jnp.cos(theta), jnp.sin(theta)], axis=1)
    phi = -phase(
        (2 * shard[:, None] * row[None, :])[None] + branch[:, None, None] * row[None, :][None],
        2 * length,
    )
    twiddle = (jnp.cos(phi), jnp.sin(phi))
    psi = -phase(row[:, None] * row[None, :], row_count)
    cos_b, sin_b = jnp.cos(psi), jnp.sin(psi)
    stage_b = jnp.stack(
        [jnp.stack([cos_b, sin_b], axis=1), jnp.stack([-sin_b, cos_b], axis=1)]
    )
    stage_b_inv = jnp.stack(
        [jnp.stack([cos_b, -sin_b], axis=1), jnp.stack([sin_b, cos_b], axis=1)]
    )
    stage_a_inv = stage_a * (0.5 / length)
    return stage_a, twiddle, stage_b, stage_b_inv, stage_a_inv


def complex_scale(value, cos_part, sin_part, axis):
    real_part = lax.index_in_dim(value, 0, axis, keepdims=False)
    imag_part = lax.index_in_dim(value, 1, axis, keepdims=False)
    return jnp.stack(
        [real_part * cos_part - imag_part * sin_part, real_part * sin_part + imag_part * cos_part],
        axis=axis,
    )


def to_columns(rows, wire=jnp.float32):
    shard_count = lax.axis_size("seq")
    batch, row_count, _ = rows.shape
    columns = lax.all_to_all(
        jnp.swapaxes(rows, 1, 2).astype(wire), "seq", split_axis=1, concat_axis=2, tiled=True
    ).astype(jnp.float32)
    return columns.reshape(batch, columns.shape[1], shard_count, row_count)


def to_rows(columns, wire=jnp.float32):
    batch, chan_count, shard_count, row_count = columns.shape
    rows = lax.all_to_all(
        columns.astype(wire), "seq", split_axis=2, concat_axis=1, tiled=True
    ).astype(jnp.float32)
    return jnp.swapaxes(rows.reshape(batch, shard_count * chan_count, row_count), 1, 2)


def forward_spectrum(columns, tables):
    stage_a, twiddle, stage_b, _, _ = tables
    spread = jnp.einsum("erkp,bcpm->bcerkm", stage_a, columns, precision=STAGE_A_PRECISION)
    spread = complex_scale(spread, twiddle[0], twiddle[1], 3)
    return jnp.einsum("bcerkm,rmsq->bceskq", spread, stage_b, precision=STAGE_B_PRECISION)


def inverse_spectrum(spectrum, tables):
    _, twiddle, _, stage_b_inv, stage_a_inv = tables
    spread = jnp.einsum("bceskq,sqrm->bcerkm", spectrum, stage_b_inv, precision=STAGE_B_PRECISION)
    spread = complex_scale(spread, twiddle[0], -twiddle[1], 3)
    return jnp.einsum("erkp,bcerkm->bcpm", stage_a_inv, spread, precision=STAGE_A_PRECISION)


def local_body(tokens, cotangent, in_weight, short_kernel, skip_gain, long_filter, out_weight):
    row_count = tokens.shape[0]
    tap_count = short_kernel.shape[0]
    shard_count = lax.axis_size("seq")
    tables = transform_tables(shard_count, row_count)
    filt_spec = forward_spectrum(to_columns(long_filter[None]), tables)
    width = tokens.shape[1]
    projected = 0.0
    token_parts = panel_parts(tokens)
    cotangent_parts = panel_parts(cotangent)
    for part, source in token_parts:
        projected = projected + jnp.einsum(
            "td,jdc->jtc",
            part,
            lax.dynamic_slice_in_dim(in_weight, source * width, width, axis=1),
            preferred_element_type=jnp.float32,
        )
    grad_gated = 0.0
    for part, source in cotangent_parts:
        grad_gated = grad_gated + lax.dot_general(
            part,
            lax.dynamic_slice_in_dim(out_weight, source * width, width, axis=1),
            (((1,), (1,)), ((), ())),
            preferred_element_type=jnp.float32,
        )
    projected = projected.astype(jnp.bfloat16)

    before = shifted(projected[:, row_count - (tap_count - 1) :, :], "seq", 1)
    extended = jnp.concatenate([before, projected], axis=1).astype(jnp.float32)
    filtered = short_kernel[0][:, None, :] * extended[:, tap_count - 1 :, :]
    for tap_index in range(1, tap_count):
        filtered = (
            filtered
            + short_kernel[tap_index][:, None, :]
            * extended[:, tap_count - 1 - tap_index : tap_count - 1 - tap_index + row_count, :]
        )
    gate_out, gate_in, value_path = (filtered[0], filtered[1], filtered[2])
    signal = value_path * gate_in
    grad_state = grad_gated * gate_out
    spectra = jnp.concatenate(
        [
            forward_spectrum(to_columns(signal[None], WIRE), tables),
            forward_spectrum(to_columns(grad_state[None], WIRE), tables),
        ]
    )
    filt_real, filt_imag = filt_spec[:, :, :, 0], filt_spec[:, :, :, 1]
    sig_real, sig_imag = spectra[0:1, :, :, 0], spectra[0:1, :, :, 1]
    grad_real, grad_imag = spectra[1:2, :, :, 0], spectra[1:2, :, :, 1]
    product = jnp.concatenate(
        [
            jnp.stack(
                [sig_real * filt_real - sig_imag * filt_imag, sig_real * filt_imag + sig_imag * filt_real],
                axis=3,
            ),
            jnp.stack(
                [grad_real * filt_real + grad_imag * filt_imag, grad_imag * filt_real - grad_real * filt_imag],
                axis=3,
            ),
        ]
    )
    convolved = to_rows(inverse_spectrum(product, tables), WIRE)
    conv_state = convolved[0] + skip_gain[None, :] * signal
    grad_signal = convolved[1] + skip_gain[None, :] * grad_state
    gated_state = (conv_state * gate_out).astype(jnp.bfloat16)
    block_out = panel_reduce_scatter(
        lambda dest: jnp.dot(
            gated_state,
            lax.dynamic_slice_in_dim(out_weight, dest * width, width, axis=1),
            preferred_element_type=jnp.float32,
        )
    )
    grad_gate_out = grad_gated * conv_state
    grad_value = grad_signal * gate_in
    grad_gate_in = grad_signal * value_path
    upstream = jnp.stack([grad_gate_out, grad_gate_in, grad_value])
    after_rim = shifted(upstream[:, : tap_count - 1, :], "seq", -1)
    widened = jnp.concatenate([upstream, after_rim], axis=1)
    grad_projected = short_kernel[0][:, None, :] * widened[:, :row_count, :]
    for tap_index in range(1, tap_count):
        grad_projected = (
            grad_projected
            + short_kernel[tap_index][:, None, :] * widened[:, tap_index : tap_index + row_count, :]
        )
    grad_projected = grad_projected.astype(jnp.bfloat16)
    token_grad = panel_reduce_scatter(
        lambda dest: jnp.einsum(
            "jtc,jdc->td",
            grad_projected,
            lax.dynamic_slice_in_dim(in_weight, dest * width, width, axis=1),
            preferred_element_type=jnp.float32,
        )
    )
    return (block_out, token_grad)


def solution(mesh):
    placed = (
        P("seq", "panel"),
        P("seq", "panel"),
        P(None, None, "panel"),
        P(None, None, "panel"),
        P("panel"),
        P("seq", "panel"),
        P("panel", None),
    )
    return jax.shard_map(
        local_body,
        mesh=mesh,
        in_specs=placed,
        out_specs=(P("seq", "panel"), P("seq", "panel")),
        check_vma=False,
    )
```

```python
import math

import jax
import jax.numpy as jnp
from jax import lax
from jax.sharding import PartitionSpec as P

HIGHEST = lax.Precision.HIGHEST
STAGE_A_PRECISION = lax.Precision.HIGHEST
STAGE_B_PRECISION = lax.Precision.HIGH
WIRE = jnp.bfloat16


def shifted(value, axis, steps):
    count = lax.axis_size(axis)
    initial, last = (max(0, -steps), min(count, count - steps))
    return lax.ppermute(value, axis, [(source, source + steps) for source in range(initial, last)])


def panel_parts(value):
    count = lax.axis_size("panel")
    me = lax.axis_index("panel")
    parts = [(value, me)]
    for k in range(1, count):
        moved = lax.ppermute(value, "panel", [(i, (i + k) % count) for i in range(count)])
        parts.append((moved, (me + count - k) % count))
    return parts


def panel_reduce_scatter(block_of):
    count = lax.axis_size("panel")
    me = lax.axis_index("panel")
    total = block_of(me)
    for k in range(1, count):
        sent = block_of((me + k) % count).astype(jnp.bfloat16)
        total = total + lax.ppermute(
            sent, "panel", [(i, (i + k) % count) for i in range(count)]
        ).astype(jnp.float32)
    return total


def halo_to_previous(halo):
    seq_count, count = lax.axis_size("seq"), lax.axis_size("panel")
    me = lax.axis_index("panel")
    rows, cols = halo.shape
    width = cols // count
    total = 0.0
    for k in range(count):
        sent = lax.dynamic_slice_in_dim(halo, ((me + k) % count) * width, width, axis=1)
        pairs = [
            (s * count + p, (s - 1) * count + (p + k) % count)
            for s in range(1, seq_count)
            for p in range(count)
        ]
        total = total + lax.ppermute(sent, ("seq", "panel"), pairs)
    return total


def phase(numer, period):
    return (2.0 * math.pi / period) * (numer % period).astype(jnp.float32)


def transform_tables(shard_count, row_count):
    length = shard_count * row_count
    branch = jnp.arange(2, dtype=jnp.int32)
    shard = jnp.arange(shard_count, dtype=jnp.int32)
    row = jnp.arange(row_count, dtype=jnp.int32)
    theta = -phase(
        (2 * shard[:, None] * shard[None, :])[None] + branch[:, None, None] * shard[None, None, :],
        2 * shard_count,
    )
    stage_a = jnp.stack([jnp.cos(theta), jnp.sin(theta)], axis=1)
    phi = -phase(
        (2 * shard[:, None] * row[None, :])[None] + branch[:, None, None] * row[None, :][None],
        2 * length,
    )
    twiddle = (jnp.cos(phi), jnp.sin(phi))
    psi = -phase(row[:, None] * row[None, :], row_count)
    cos_b, sin_b = jnp.cos(psi), jnp.sin(psi)
    stage_b = jnp.stack(
        [jnp.stack([cos_b, sin_b], axis=1), jnp.stack([-sin_b, cos_b], axis=1)]
    )
    stage_b_inv = jnp.stack(
        [jnp.stack([cos_b, -sin_b], axis=1), jnp.stack([sin_b, cos_b], axis=1)]
    )
    stage_a_inv = stage_a * (0.5 / length)
    return stage_a, twiddle, stage_b, stage_b_inv, stage_a_inv


def complex_scale(value, cos_part, sin_part, axis):
    real_part = lax.index_in_dim(value, 0, axis, keepdims=False)
    imag_part = lax.index_in_dim(value, 1, axis, keepdims=False)
    return jnp.stack(
        [real_part * cos_part - imag_part * sin_part, real_part * sin_part + imag_part * cos_part],
        axis=axis,
    )


def to_columns(rows, wire=jnp.float32):
    shard_count = lax.axis_size("seq")
    batch, row_count, _ = rows.shape
    columns = lax.all_to_all(
        jnp.swapaxes(rows, 1, 2).astype(wire), "seq", split_axis=1, concat_axis=2, tiled=True
    ).astype(jnp.float32)
    return columns.reshape(batch, columns.shape[1], shard_count, row_count)


def to_rows(columns, wire=jnp.float32):
    batch, chan_count, shard_count, row_count = columns.shape
    rows = lax.all_to_all(
        columns.astype(wire), "seq", split_axis=2, concat_axis=1, tiled=True
    ).astype(jnp.float32)
    return jnp.swapaxes(rows.reshape(batch, shard_count * chan_count, row_count), 1, 2)


def forward_spectrum(columns, tables):
    stage_a, twiddle, stage_b, _, _ = tables
    spread = jnp.einsum("erkp,bcpm->bcerkm", stage_a, columns, precision=STAGE_A_PRECISION)
    spread = complex_scale(spread, twiddle[0], twiddle[1], 3)
    return jnp.einsum("bcerkm,rmsq->bceskq", spread, stage_b, precision=STAGE_B_PRECISION)


def inverse_spectrum(spectrum, tables):
    _, twiddle, _, stage_b_inv, stage_a_inv = tables
    spread = jnp.einsum("bceskq,sqrm->bcerkm", spectrum, stage_b_inv, precision=STAGE_B_PRECISION)
    spread = complex_scale(spread, twiddle[0], -twiddle[1], 3)
    return jnp.einsum("erkp,bcerkm->bcpm", stage_a_inv, spread, precision=STAGE_A_PRECISION)


def local(tokens, cotangent, in_weight, short_kernel, skip_gain, long_filter, out_weight):
    row_count = tokens.shape[0]
    tap_count = short_kernel.shape[0]
    shard_count = lax.axis_size("seq")
    tables = transform_tables(shard_count, row_count)
    filt_spec = forward_spectrum(to_columns(long_filter[None]), tables)
    width = tokens.shape[1]
    projected = 0.0
    for part, source in panel_parts(tokens):
        projected = projected + jnp.einsum(
            "td,jdc->jtc",
            part,
            lax.dynamic_slice_in_dim(in_weight, source * width, width, axis=1),
            preferred_element_type=jnp.float32,
        )
    grad_gated = 0.0
    for part, source in panel_parts(cotangent):
        grad_gated = grad_gated + lax.dot_general(
            part,
            lax.dynamic_slice_in_dim(out_weight, source * width, width, axis=1),
            (((1,), (1,)), ((), ())),
            preferred_element_type=jnp.float32,
        )
    projected = projected.astype(jnp.bfloat16)

    before = shifted(projected[:, row_count - (tap_count - 1) :, :], "seq", 1)
    extended = jnp.concatenate([before, projected], axis=1).astype(jnp.float32)
    filtered = short_kernel[0][:, None, :] * extended[:, tap_count - 1 :, :]
    for tap_index in range(1, tap_count):
        filtered = (
            filtered
            + short_kernel[tap_index][:, None, :]
            * extended[:, tap_count - 1 - tap_index : tap_count - 1 - tap_index + row_count, :]
        )
    gate_out, gate_in, value_path = (filtered[0], filtered[1], filtered[2])
    signal = value_path * gate_in
    grad_state = grad_gated * gate_out
    spectra = forward_spectrum(to_columns(jnp.stack([signal, grad_state]), WIRE), tables)
    filt_real, filt_imag = filt_spec[:, :, :, 0], filt_spec[:, :, :, 1]
    sig_real, sig_imag = spectra[0:1, :, :, 0], spectra[0:1, :, :, 1]
    grad_real, grad_imag = spectra[1:2, :, :, 0], spectra[1:2, :, :, 1]
    product = jnp.concatenate(
        [
            jnp.stack(
                [sig_real * filt_real - sig_imag * filt_imag, sig_real * filt_imag + sig_imag * filt_real],
                axis=3,
            ),
            jnp.stack(
                [grad_real * filt_real + grad_imag * filt_imag, grad_imag * filt_real - grad_real * filt_imag],
                axis=3,
            ),
        ]
    )
    convolved = to_rows(inverse_spectrum(product, tables), WIRE)
    conv_state = convolved[0] + skip_gain[None, :] * signal
    grad_signal = convolved[1] + skip_gain[None, :] * grad_state
    gated_state = (conv_state * gate_out).astype(jnp.bfloat16)
    block_out = panel_reduce_scatter(
        lambda dest: jnp.dot(
            gated_state,
            lax.dynamic_slice_in_dim(out_weight, dest * width, width, axis=1),
            preferred_element_type=jnp.float32,
        )
    ).astype(jnp.bfloat16)
    grad_gate_out = grad_gated * conv_state
    grad_value = grad_signal * gate_in
    grad_gate_in = grad_signal * value_path
    upstream = jnp.stack([grad_gate_out, grad_gate_in, grad_value])
    rim = tap_count - 1
    halo_proj = jnp.stack(
        [
            sum(
                short_kernel[tap_index][:, None, :]
                * upstream[:, tap_index - rim + rim_row : tap_index - rim + rim_row + 1, :]
                for tap_index in range(rim - rim_row, tap_count)
            )[:, 0, :]
            for rim_row in range(rim)
        ],
        axis=1,
    )
    halo_grad = jnp.einsum(
        "jrc,jdc->rd",
        halo_proj,
        in_weight.astype(jnp.float32),
        precision=HIGHEST,
        preferred_element_type=jnp.float32,
    )
    halo_in = halo_to_previous(halo_grad)
    grad_projected = short_kernel[0][:, None, :] * upstream
    for tap_index in range(1, tap_count):
        grad_projected = grad_projected + short_kernel[tap_index][:, None, :] * jnp.pad(
            upstream[:, tap_index:, :], ((0, 0), (0, tap_index), (0, 0))
        )
    grad_projected = grad_projected.astype(jnp.bfloat16)
    token_grad = panel_reduce_scatter(
        lambda dest: jnp.einsum(
            "jtc,jdc->td",
            grad_projected,
            lax.dynamic_slice_in_dim(in_weight, dest * width, width, axis=1),
            preferred_element_type=jnp.float32,
        )
    )
    token_grad = jnp.concatenate(
        [token_grad[: row_count - rim], token_grad[row_count - rim :] + halo_in]
    ).astype(jnp.bfloat16)
    return (block_out, token_grad)


def solution(mesh):
    placed = (
        P("seq", "panel"),
        P("seq", "panel"),
        P(None, None, "panel"),
        P(None, None, "panel"),
        P("panel"),
        P("seq", "panel"),
        P("panel", None),
    )
    return jax.shard_map(
        local,
        mesh=mesh,
        in_specs=placed,
        out_specs=(P("seq", "panel"), P("seq", "panel")),
        check_vma=False,
    )
```

```python
import math

import jax
import jax.numpy as jnp
from jax import lax
from jax.sharding import PartitionSpec as P

HIGHEST = lax.Precision.HIGHEST
STAGE_A_PRECISION = lax.Precision.HIGH
STAGE_B_PRECISION = lax.Precision.HIGH
WIRE = jnp.bfloat16


def shifted(value, axis, steps):
    count = lax.axis_size(axis)
    initial, last = (max(0, -steps), min(count, count - steps))
    return lax.ppermute(value, axis, [(source, source + steps) for source in range(initial, last)])


def panel_parts(value):
    count = lax.axis_size("panel")
    me = lax.axis_index("panel")
    parts = [(value, me)]
    for k in range(1, count):
        moved = lax.ppermute(value, "panel", [(i, (i + k) % count) for i in range(count)])
        parts.append((moved, (me + count - k) % count))
    return parts


def panel_reduce_scatter(block_of):
    count = lax.axis_size("panel")
    me = lax.axis_index("panel")
    total = block_of(me)
    for k in range(1, count):
        sent = block_of((me + k) % count).astype(jnp.bfloat16)
        total = total + lax.ppermute(
            sent, "panel", [(i, (i + k) % count) for i in range(count)]
        ).astype(jnp.float32)
    return total.astype(jnp.bfloat16)


def phase(numer, period):
    return (2.0 * math.pi / period) * (numer % period).astype(jnp.float32)


def transform_tables(shard_count, row_count):
    length = shard_count * row_count
    branch = jnp.arange(2, dtype=jnp.int32)
    shard = jnp.arange(shard_count, dtype=jnp.int32)
    row = jnp.arange(row_count, dtype=jnp.int32)
    theta = -phase(
        (2 * shard[:, None] * shard[None, :])[None] + branch[:, None, None] * shard[None, None, :],
        2 * shard_count,
    )
    stage_a = jnp.stack([jnp.cos(theta), jnp.sin(theta)], axis=1)
    phi = -phase(
        (2 * shard[:, None] * row[None, :])[None] + branch[:, None, None] * row[None, :][None],
        2 * length,
    )
    twiddle = (jnp.cos(phi), jnp.sin(phi))
    psi = -phase(row[:, None] * row[None, :], row_count)
    cos_b, sin_b = jnp.cos(psi), jnp.sin(psi)
    stage_b = jnp.stack(
        [jnp.stack([cos_b, sin_b], axis=1), jnp.stack([-sin_b, cos_b], axis=1)]
    )
    stage_b_inv = jnp.stack(
        [jnp.stack([cos_b, -sin_b], axis=1), jnp.stack([sin_b, cos_b], axis=1)]
    )
    stage_a_inv = stage_a * (0.5 / length)
    return stage_a, twiddle, stage_b, stage_b_inv, stage_a_inv


def complex_scale(value, cos_part, sin_part, axis):
    real_part = lax.index_in_dim(value, 0, axis, keepdims=False)
    imag_part = lax.index_in_dim(value, 1, axis, keepdims=False)
    return jnp.stack(
        [real_part * cos_part - imag_part * sin_part, real_part * sin_part + imag_part * cos_part],
        axis=axis,
    )


def to_columns(rows, wire=jnp.float32):
    shard_count = lax.axis_size("seq")
    batch, row_count, _ = rows.shape
    columns = lax.all_to_all(
        jnp.swapaxes(rows, 1, 2).astype(wire), "seq", split_axis=1, concat_axis=2, tiled=True
    ).astype(jnp.float32)
    return columns.reshape(batch, columns.shape[1], shard_count, row_count)


def to_rows(columns, wire=jnp.float32):
    batch, chan_count, shard_count, row_count = columns.shape
    rows = lax.all_to_all(
        columns.astype(wire), "seq", split_axis=2, concat_axis=1, tiled=True
    ).astype(jnp.float32)
    return jnp.swapaxes(rows.reshape(batch, shard_count * chan_count, row_count), 1, 2)


def forward_spectrum(columns, tables):
    stage_a, twiddle, stage_b, _, _ = tables
    spread = jnp.einsum("erkp,bcpm->bcerkm", stage_a, columns, precision=STAGE_A_PRECISION)
    spread = complex_scale(spread, twiddle[0], twiddle[1], 3)
    return jnp.einsum("bcerkm,rmsq->bceskq", spread, stage_b, precision=STAGE_B_PRECISION)


def inverse_spectrum(spectrum, tables):
    _, twiddle, _, stage_b_inv, stage_a_inv = tables
    spread = jnp.einsum("bceskq,sqrm->bcerkm", spectrum, stage_b_inv, precision=STAGE_B_PRECISION)
    spread = complex_scale(spread, twiddle[0], -twiddle[1], 3)
    return jnp.einsum("erkp,bcerkm->bcpm", stage_a_inv, spread, precision=STAGE_A_PRECISION)


def local(tokens, cotangent, in_weight, short_kernel, skip_gain, long_filter, out_weight):
    row_count = tokens.shape[0]
    tap_count = short_kernel.shape[0]
    shard_count = lax.axis_size("seq")
    tables = transform_tables(shard_count, row_count)
    filt_spec = forward_spectrum(to_columns(long_filter[None]), tables)
    width = tokens.shape[1]
    projected = 0.0
    for part, source in panel_parts(tokens):
        projected = projected + jnp.einsum(
            "td,jdc->jtc",
            part,
            lax.dynamic_slice_in_dim(in_weight, source * width, width, axis=1),
            preferred_element_type=jnp.float32,
        )
    grad_gated = 0.0
    for part, source in panel_parts(cotangent):
        grad_gated = grad_gated + lax.dot_general(
            part,
            lax.dynamic_slice_in_dim(out_weight, source * width, width, axis=1),
            (((1,), (1,)), ((), ())),
            preferred_element_type=jnp.float32,
        )
    projected = projected.astype(jnp.bfloat16)

    before = shifted(projected[:, row_count - (tap_count - 1) :, :], "seq", 1)
    extended = jnp.concatenate([before, projected], axis=1).astype(jnp.float32)
    filtered = short_kernel[0][:, None, :] * extended[:, tap_count - 1 :, :]
    for tap_index in range(1, tap_count):
        filtered = (
            filtered
            + short_kernel[tap_index][:, None, :]
            * extended[:, tap_count - 1 - tap_index : tap_count - 1 - tap_index + row_count, :]
        )
    gate_out, gate_in, value_path = (filtered[0], filtered[1], filtered[2])
    signal = value_path * gate_in
    grad_state = grad_gated * gate_out
    spectra = forward_spectrum(to_columns(jnp.stack([signal, grad_state]), WIRE), tables)
    filt_real, filt_imag = filt_spec[:, :, :, 0], filt_spec[:, :, :, 1]
    sig_real, sig_imag = spectra[0:1, :, :, 0], spectra[0:1, :, :, 1]
    grad_real, grad_imag = spectra[1:2, :, :, 0], spectra[1:2, :, :, 1]
    product = jnp.concatenate(
        [
            jnp.stack(
                [sig_real * filt_real - sig_imag * filt_imag, sig_real * filt_imag + sig_imag * filt_real],
                axis=3,
            ),
            jnp.stack(
                [grad_real * filt_real + grad_imag * filt_imag, grad_imag * filt_real - grad_real * filt_imag],
                axis=3,
            ),
        ]
    )
    convolved = to_rows(inverse_spectrum(product, tables), WIRE)
    conv_state = convolved[0] + skip_gain[None, :] * signal
    grad_signal = convolved[1] + skip_gain[None, :] * grad_state
    gated_state = (conv_state * gate_out).astype(jnp.bfloat16)
    block_out = panel_reduce_scatter(
        lambda dest: jnp.dot(
            gated_state,
            lax.dynamic_slice_in_dim(out_weight, dest * width, width, axis=1),
            preferred_element_type=jnp.float32,
        )
    )
    grad_gate_out = grad_gated * conv_state
    grad_value = grad_signal * gate_in
    grad_gate_in = grad_signal * value_path
    upstream = jnp.stack([grad_gate_out, grad_gate_in, grad_value])
    after_rim = shifted(upstream[:, : tap_count - 1, :], "seq", -1)
    widened = jnp.concatenate([upstream, after_rim], axis=1)
    grad_projected = short_kernel[0][:, None, :] * widened[:, :row_count, :]
    for tap_index in range(1, tap_count):
        grad_projected = (
            grad_projected
            + short_kernel[tap_index][:, None, :] * widened[:, tap_index : tap_index + row_count, :]
        )
    grad_projected = grad_projected.astype(jnp.bfloat16)
    token_grad = panel_reduce_scatter(
        lambda dest: jnp.einsum(
            "jtc,jdc->td",
            grad_projected,
            lax.dynamic_slice_in_dim(in_weight, dest * width, width, axis=1),
            preferred_element_type=jnp.float32,
        )
    )
    return (block_out, token_grad)


def solution(mesh):
    placed = (
        P("seq", "panel"),
        P("seq", "panel"),
        P(None, None, "panel"),
        P(None, None, "panel"),
        P("panel"),
        P("seq", "panel"),
        P("panel", None),
    )
    return jax.shard_map(
        local,
        mesh=mesh,
        in_specs=placed,
        out_specs=(P("seq", "panel"), P("seq", "panel")),
        check_vma=False,
    )
```

```python
import math

import jax
import jax.numpy as jnp
from jax import lax
from jax.sharding import PartitionSpec as P

HIGHEST = lax.Precision.HIGHEST
STAGE_A_PRECISION = lax.Precision.HIGH
STAGE_B_PRECISION = lax.Precision.HIGH
WIRE = jnp.bfloat16


def shifted(value, axis, steps):
    count = lax.axis_size(axis)
    initial, last = (max(0, -steps), min(count, count - steps))
    return lax.ppermute(value, axis, [(source, source + steps) for source in range(initial, last)])


def panel_parts(value):
    count = lax.axis_size("panel")
    me = lax.axis_index("panel")
    parts = [(value, me)]
    for k in range(1, count):
        moved = lax.ppermute(value, "panel", [(i, (i + k) % count) for i in range(count)])
        parts.append((moved, (me + count - k) % count))
    return parts


def panel_reduce_scatter(block_of):
    count = lax.axis_size("panel")
    me = lax.axis_index("panel")
    total = block_of(me)
    for k in range(1, count):
        sent = block_of((me + k) % count).astype(jnp.bfloat16)
        total = total + lax.ppermute(
            sent, "panel", [(i, (i + k) % count) for i in range(count)]
        ).astype(jnp.float32)
    return total.astype(jnp.bfloat16)


def phase(numer, period):
    return (2.0 * math.pi / period) * (numer % period).astype(jnp.float32)


def transform_tables(shard_count, row_count):
    length = shard_count * row_count
    branch = jnp.arange(2, dtype=jnp.int32)
    shard = jnp.arange(shard_count, dtype=jnp.int32)
    row = jnp.arange(row_count, dtype=jnp.int32)
    theta = -phase(
        (2 * shard[:, None] * shard[None, :])[None] + branch[:, None, None] * shard[None, None, :],
        2 * shard_count,
    )
    stage_a = jnp.stack([jnp.cos(theta), jnp.sin(theta)], axis=1)
    phi = -phase(
        (2 * shard[:, None] * row[None, :])[None] + branch[:, None, None] * row[None, :][None],
        2 * length,
    )
    twiddle = (jnp.cos(phi), jnp.sin(phi))
    psi = -phase(row[:, None] * row[None, :], row_count)
    cos_b, sin_b = jnp.cos(psi), jnp.sin(psi)
    stage_b = jnp.stack(
        [jnp.stack([cos_b, sin_b], axis=1), jnp.stack([-sin_b, cos_b], axis=1)]
    )
    stage_b_inv = jnp.stack(
        [jnp.stack([cos_b, -sin_b], axis=1), jnp.stack([sin_b, cos_b], axis=1)]
    )
    stage_a_inv = stage_a * (0.5 / length)
    return stage_a, twiddle, stage_b, stage_b_inv, stage_a_inv


def complex_scale(value, cos_part, sin_part, axis):
    real_part = lax.index_in_dim(value, 0, axis, keepdims=False)
    imag_part = lax.index_in_dim(value, 1, axis, keepdims=False)
    return jnp.stack(
        [real_part * cos_part - imag_part * sin_part, real_part * sin_part + imag_part * cos_part],
        axis=axis,
    )


def to_columns(rows, wire=jnp.float32):
    shard_count = lax.axis_size("seq")
    batch, row_count, _ = rows.shape
    columns = lax.all_to_all(
        jnp.swapaxes(rows, 1, 2).astype(wire), "seq", split_axis=1, concat_axis=2, tiled=True
    ).astype(jnp.float32)
    return columns.reshape(batch, columns.shape[1], shard_count, row_count)


def to_rows(columns, wire=jnp.float32):
    batch, chan_count, shard_count, row_count = columns.shape
    rows = lax.all_to_all(
        columns.astype(wire), "seq", split_axis=2, concat_axis=1, tiled=True
    ).astype(jnp.float32)
    return jnp.swapaxes(rows.reshape(batch, shard_count * chan_count, row_count), 1, 2)


def forward_spectrum(columns, tables):
    stage_a, twiddle, stage_b, _, _ = tables
    spread = jnp.einsum("erkp,bcpm->bcerkm", stage_a, columns, precision=STAGE_A_PRECISION)
    spread = complex_scale(spread, twiddle[0], twiddle[1], 3)
    return jnp.einsum("bcerkm,rmsq->bceskq", spread, stage_b, precision=STAGE_B_PRECISION)


def forward_packed(columns, tables):
    stage_a, twiddle, stage_b, _, _ = tables
    packed_a = jnp.stack(
        [stage_a, jnp.stack([-stage_a[:, 1], stage_a[:, 0]], axis=1)], axis=3
    )
    spread = jnp.einsum("erkip,icpm->cerkm", packed_a, columns, precision=STAGE_A_PRECISION)
    spread = complex_scale(spread[None], twiddle[0], twiddle[1], 3)
    return jnp.einsum("bcerkm,rmsq->bceskq", spread, stage_b, precision=STAGE_B_PRECISION)


def reversed_conjugate(spectrum):
    shard_count = spectrum.shape[4]
    even, odd = spectrum[:, :, 0], spectrum[:, :, 1]
    odd_rev = jnp.flip(odd, axis=(-2, -1))
    even_k = jnp.roll(jnp.flip(even, axis=-2), 1, axis=-2)
    even_q = jnp.flip(even_k, axis=-1)
    first_row = (jnp.arange(shard_count) == 0)[:, None]
    even_rev = jnp.where(first_row, jnp.roll(even_q, 1, axis=-1), even_q)
    rev = jnp.stack([even_rev, odd_rev], axis=2)
    return jnp.stack([rev[:, :, :, 0], -rev[:, :, :, 1]], axis=3)


def inverse_packed(spectrum, tables):
    _, twiddle, _, stage_b_inv, stage_a_inv = tables
    spread = jnp.einsum("bceskq,sqrm->bcerkm", spectrum, stage_b_inv, precision=STAGE_B_PRECISION)
    spread = complex_scale(spread, twiddle[0], -twiddle[1], 3)
    packed_a = jnp.stack(
        [stage_a_inv, jnp.stack([-stage_a_inv[:, 1], stage_a_inv[:, 0]], axis=1)]
    )
    return jnp.einsum("oerkp,bcerkm->obcpm", packed_a, spread, precision=STAGE_A_PRECISION)


def inverse_spectrum(spectrum, tables):
    _, twiddle, _, stage_b_inv, stage_a_inv = tables
    spread = jnp.einsum("bceskq,sqrm->bcerkm", spectrum, stage_b_inv, precision=STAGE_B_PRECISION)
    spread = complex_scale(spread, twiddle[0], -twiddle[1], 3)
    return jnp.einsum("erkp,bcerkm->bcpm", stage_a_inv, spread, precision=STAGE_A_PRECISION)


def local(tokens, cotangent, in_weight, short_kernel, skip_gain, long_filter, out_weight):
    row_count = tokens.shape[0]
    tap_count = short_kernel.shape[0]
    shard_count = lax.axis_size("seq")
    tables = transform_tables(shard_count, row_count)
    filt_spec = forward_spectrum(to_columns(long_filter[None]), tables)
    width = tokens.shape[1]
    projected = 0.0
    for part, source in panel_parts(tokens):
        projected = projected + jnp.einsum(
            "td,jdc->jtc",
            part,
            lax.dynamic_slice_in_dim(in_weight, source * width, width, axis=1),
            preferred_element_type=jnp.float32,
        )
    grad_gated = 0.0
    for part, source in panel_parts(cotangent):
        grad_gated = grad_gated + lax.dot_general(
            part,
            lax.dynamic_slice_in_dim(out_weight, source * width, width, axis=1),
            (((1,), (1,)), ((), ())),
            preferred_element_type=jnp.float32,
        )
    projected = projected.astype(jnp.bfloat16)

    before = shifted(projected[:, row_count - (tap_count - 1) :, :], "seq", 1)
    extended = jnp.concatenate([before, projected], axis=1).astype(jnp.float32)
    filtered = short_kernel[0][:, None, :] * extended[:, tap_count - 1 :, :]
    for tap_index in range(1, tap_count):
        filtered = (
            filtered
            + short_kernel[tap_index][:, None, :]
            * extended[:, tap_count - 1 - tap_index : tap_count - 1 - tap_index + row_count, :]
        )
    gate_out, gate_in, value_path = (filtered[0], filtered[1], filtered[2])
    signal = value_path * gate_in
    grad_state = grad_gated * gate_out
    spectrum = forward_packed(to_columns(jnp.stack([signal, grad_state]), WIRE), tables)
    mirrored = reversed_conjugate(spectrum)
    filt_real, filt_imag = filt_spec[:, :, :, 0], filt_spec[:, :, :, 1]
    product = jnp.stack(
        [
            spectrum[:, :, :, 0] * filt_real - mirrored[:, :, :, 1] * filt_imag,
            spectrum[:, :, :, 1] * filt_real + mirrored[:, :, :, 0] * filt_imag,
        ],
        axis=3,
    )
    convolved = to_rows(inverse_packed(product, tables)[:, 0], WIRE)
    conv_state = convolved[0] + skip_gain[None, :] * signal
    grad_signal = convolved[1] + skip_gain[None, :] * grad_state
    gated_state = (conv_state * gate_out).astype(jnp.bfloat16)
    block_out = panel_reduce_scatter(
        lambda dest: jnp.dot(
            gated_state,
            lax.dynamic_slice_in_dim(out_weight, dest * width, width, axis=1),
            preferred_element_type=jnp.float32,
        )
    )
    grad_gate_out = grad_gated * conv_state
    grad_value = grad_signal * gate_in
    grad_gate_in = grad_signal * value_path
    upstream = jnp.stack([grad_gate_out, grad_gate_in, grad_value])
    after_rim = shifted(upstream[:, : tap_count - 1, :], "seq", -1)
    widened = jnp.concatenate([upstream, after_rim], axis=1)
    grad_projected = short_kernel[0][:, None, :] * widened[:, :row_count, :]
    for tap_index in range(1, tap_count):
        grad_projected = (
            grad_projected
            + short_kernel[tap_index][:, None, :] * widened[:, tap_index : tap_index + row_count, :]
        )
    grad_projected = grad_projected.astype(jnp.bfloat16)
    token_grad = panel_reduce_scatter(
        lambda dest: jnp.einsum(
            "jtc,jdc->td",
            grad_projected,
            lax.dynamic_slice_in_dim(in_weight, dest * width, width, axis=1),
            preferred_element_type=jnp.float32,
        )
    )
    return (block_out, token_grad)


def solution(mesh):
    placed = (
        P("seq", "panel"),
        P("seq", "panel"),
        P(None, None, "panel"),
        P(None, None, "panel"),
        P("panel"),
        P("seq", "panel"),
        P("panel", None),
    )
    return jax.shard_map(
        local,
        mesh=mesh,
        in_specs=placed,
        out_specs=(P("seq", "panel"), P("seq", "panel")),
        check_vma=False,
    )
```

```python
import math

import jax
import jax.numpy as jnp
from jax import lax
from jax.sharding import PartitionSpec as P

HIGHEST = lax.Precision.HIGHEST
STAGE_A_PRECISION = lax.Precision.HIGH
STAGE_B_PRECISION = lax.Precision.HIGH
WIRE = jnp.bfloat16
EDGE = 16


def shifted(value, axis, steps):
    count = lax.axis_size(axis)
    initial, last = (max(0, -steps), min(count, count - steps))
    return lax.ppermute(value, axis, [(source, source + steps) for source in range(initial, last)])


def panel_parts(value):
    count = lax.axis_size("panel")
    me = lax.axis_index("panel")
    parts = [(value, me)]
    for k in range(1, count):
        moved = lax.ppermute(value, "panel", [(i, (i + k) % count) for i in range(count)])
        parts.append((moved, (me + count - k) % count))
    return parts


def panel_reduce_scatter(block_of):
    count = lax.axis_size("panel")
    me = lax.axis_index("panel")
    total = block_of(me)
    for k in range(1, count):
        sent = block_of((me + k) % count).astype(jnp.bfloat16)
        total = total + lax.ppermute(
            sent, "panel", [(i, (i + k) % count) for i in range(count)]
        ).astype(jnp.float32)
    return total.astype(jnp.bfloat16)


def phase(numer, period):
    return (2.0 * math.pi / period) * (numer % period).astype(jnp.float32)


def transform_tables(shard_count, row_count):
    length = shard_count * row_count
    branch = jnp.arange(2, dtype=jnp.int32)
    shard = jnp.arange(shard_count, dtype=jnp.int32)
    row = jnp.arange(row_count, dtype=jnp.int32)
    theta = -phase(
        (2 * shard[:, None] * shard[None, :])[None] + branch[:, None, None] * shard[None, None, :],
        2 * shard_count,
    )
    stage_a = jnp.stack([jnp.cos(theta), jnp.sin(theta)], axis=1)
    phi = -phase(
        (2 * shard[:, None] * row[None, :])[None] + branch[:, None, None] * row[None, :][None],
        2 * length,
    )
    twiddle = (jnp.cos(phi), jnp.sin(phi))
    psi = -phase(row[:, None] * row[None, :], row_count)
    cos_b, sin_b = jnp.cos(psi), jnp.sin(psi)
    stage_b = jnp.stack(
        [jnp.stack([cos_b, sin_b], axis=1), jnp.stack([-sin_b, cos_b], axis=1)]
    )
    stage_b_inv = jnp.stack(
        [jnp.stack([cos_b, -sin_b], axis=1), jnp.stack([sin_b, cos_b], axis=1)]
    )
    stage_a_inv = stage_a * (0.5 / length)
    return stage_a, twiddle, stage_b, stage_b_inv, stage_a_inv


def complex_scale(value, cos_part, sin_part, axis):
    real_part = lax.index_in_dim(value, 0, axis, keepdims=False)
    imag_part = lax.index_in_dim(value, 1, axis, keepdims=False)
    return jnp.stack(
        [real_part * cos_part - imag_part * sin_part, real_part * sin_part + imag_part * cos_part],
        axis=axis,
    )


def to_columns(rows, wire=jnp.float32):
    shard_count = lax.axis_size("seq")
    batch, row_count, _ = rows.shape
    columns = lax.all_to_all(
        jnp.swapaxes(rows, 1, 2).astype(wire), "seq", split_axis=1, concat_axis=2, tiled=True
    ).astype(jnp.float32)
    return columns.reshape(batch, columns.shape[1], shard_count, row_count)


def to_rows(columns, wire=jnp.float32):
    batch, chan_count, shard_count, row_count = columns.shape
    rows = lax.all_to_all(
        columns.astype(wire), "seq", split_axis=2, concat_axis=1, tiled=True
    ).astype(jnp.float32)
    return jnp.swapaxes(rows.reshape(batch, shard_count * chan_count, row_count), 1, 2)


def forward_spectrum(columns, tables):
    stage_a, twiddle, stage_b, _, _ = tables
    spread = jnp.einsum("erkp,bcpm->bcerkm", stage_a, columns, precision=STAGE_A_PRECISION)
    spread = complex_scale(spread, twiddle[0], twiddle[1], 3)
    return jnp.einsum("bcerkm,rmsq->bceskq", spread, stage_b, precision=STAGE_B_PRECISION)


def inverse_spectrum(spectrum, tables):
    _, twiddle, _, stage_b_inv, stage_a_inv = tables
    spread = jnp.einsum("bceskq,sqrm->bcerkm", spectrum, stage_b_inv, precision=STAGE_B_PRECISION)
    spread = complex_scale(spread, twiddle[0], -twiddle[1], 3)
    return jnp.einsum("erkp,bcerkm->bcpm", stage_a_inv, spread, precision=STAGE_A_PRECISION)


def local(tokens, cotangent, in_weight, short_kernel, skip_gain, long_filter, out_weight):
    row_count = tokens.shape[0]
    tap_count = short_kernel.shape[0]
    shard_count = lax.axis_size("seq")
    tables = transform_tables(shard_count, row_count)
    filt_spec = forward_spectrum(to_columns(long_filter[None]), tables)
    width = tokens.shape[1]
    projected = 0.0
    for part, source in panel_parts(tokens):
        projected = projected + jnp.einsum(
            "td,jdc->jtc",
            part,
            lax.dynamic_slice_in_dim(in_weight, source * width, width, axis=1),
            preferred_element_type=jnp.float32,
        )
    grad_gated = 0.0
    for part, source in panel_parts(cotangent):
        grad_gated = grad_gated + lax.dot_general(
            part,
            lax.dynamic_slice_in_dim(out_weight, source * width, width, axis=1),
            (((1,), (1,)), ((), ())),
            preferred_element_type=jnp.float32,
        )
    projected = projected.astype(jnp.bfloat16)

    before = shifted(projected[:, row_count - (tap_count - 1) :, :], "seq", 1)
    extended = jnp.concatenate([before, projected], axis=1).astype(jnp.float32)
    filtered = short_kernel[0][:, None, :] * extended[:, tap_count - 1 :, :]
    for tap_index in range(1, tap_count):
        filtered = (
            filtered
            + short_kernel[tap_index][:, None, :]
            * extended[:, tap_count - 1 - tap_index : tap_count - 1 - tap_index + row_count, :]
        )
    gate_out, gate_in, value_path = (filtered[0], filtered[1], filtered[2])
    signal = value_path * gate_in
    grad_state = grad_gated * gate_out
    spectra = forward_spectrum(to_columns(jnp.stack([signal, grad_state]), WIRE), tables)
    filt_real, filt_imag = filt_spec[:, :, :, 0], filt_spec[:, :, :, 1]
    sig_real, sig_imag = spectra[0:1, :, :, 0], spectra[0:1, :, :, 1]
    grad_real, grad_imag = spectra[1:2, :, :, 0], spectra[1:2, :, :, 1]
    product = jnp.concatenate(
        [
            jnp.stack(
                [sig_real * filt_real - sig_imag * filt_imag, sig_real * filt_imag + sig_imag * filt_real],
                axis=3,
            ),
            jnp.stack(
                [grad_real * filt_real + grad_imag * filt_imag, grad_imag * filt_real - grad_real * filt_imag],
                axis=3,
            ),
        ]
    )
    convolved = to_rows(inverse_spectrum(product, tables), WIRE)
    conv_state = convolved[0] + skip_gain[None, :] * signal
    grad_signal = convolved[1] + skip_gain[None, :] * grad_state
    gated_state = (conv_state * gate_out).astype(jnp.bfloat16)
    block_out = panel_reduce_scatter(
        lambda dest: jnp.dot(
            gated_state,
            lax.dynamic_slice_in_dim(out_weight, dest * width, width, axis=1),
            preferred_element_type=jnp.float32,
        )
    )
    grad_gate_out = grad_gated * conv_state
    grad_value = grad_signal * gate_in
    grad_gate_in = grad_signal * value_path
    upstream = jnp.stack([grad_gate_out, grad_gate_in, grad_value])
    after_rim = shifted(upstream[:, : tap_count - 1, :], "seq", -1)
    inner_rows = row_count - EDGE

    def short_taps(source, count):
        total = short_kernel[0][:, None, :] * source[:, :count, :]
        for tap_index in range(1, tap_count):
            total = total + short_kernel[tap_index][:, None, :] * source[:, tap_index : tap_index + count, :]
        return total.astype(jnp.bfloat16)

    def reduced(grad_rows):
        return panel_reduce_scatter(
            lambda dest: jnp.einsum(
                "jtc,jdc->td",
                grad_rows,
                lax.dynamic_slice_in_dim(in_weight, dest * width, width, axis=1),
                preferred_element_type=jnp.float32,
            )
        )

    inner = reduced(short_taps(upstream, inner_rows))
    edge = reduced(
        short_taps(jnp.concatenate([upstream[:, inner_rows:, :], after_rim], axis=1), EDGE)
    )
    token_grad = jnp.concatenate([inner, edge], axis=0)
    return (block_out, token_grad)


def solution(mesh):
    placed = (
        P("seq", "panel"),
        P("seq", "panel"),
        P(None, None, "panel"),
        P(None, None, "panel"),
        P("panel"),
        P("seq", "panel"),
        P("panel", None),
    )
    return jax.shard_map(
        local,
        mesh=mesh,
        in_specs=placed,
        out_specs=(P("seq", "panel"), P("seq", "panel")),
        check_vma=False,
    )
```

```python
import math

import jax
import jax.numpy as jnp
from jax import lax
from jax.sharding import PartitionSpec as P

HIGHEST = lax.Precision.HIGHEST
STAGE_A_PRECISION = lax.Precision.HIGH
STAGE_B_PRECISION = lax.Precision.HIGH
WIRE = jnp.bfloat16


def shifted(value, axis, steps):
    count = lax.axis_size(axis)
    initial, last = (max(0, -steps), min(count, count - steps))
    return lax.ppermute(value, axis, [(source, source + steps) for source in range(initial, last)])


def panel_parts(value):
    count = lax.axis_size("panel")
    me = lax.axis_index("panel")
    parts = [(value, me)]
    for k in range(1, count):
        moved = lax.ppermute(value, "panel", [(i, (i + k) % count) for i in range(count)])
        parts.append((moved, (me + count - k) % count))
    return parts


def panel_reduce_scatter(block_of):
    count = lax.axis_size("panel")
    me = lax.axis_index("panel")
    total = block_of(me)
    for k in range(1, count):
        sent = block_of((me + k) % count).astype(jnp.bfloat16)
        total = total + lax.ppermute(
            sent, "panel", [(i, (i + k) % count) for i in range(count)]
        ).astype(jnp.float32)
    return total.astype(jnp.bfloat16)


def phase(numer, period):
    return (2.0 * math.pi / period) * (numer % period).astype(jnp.float32)


def transform_tables(shard_count, row_count):
    length = shard_count * row_count
    branch = jnp.arange(2, dtype=jnp.int32)
    shard = jnp.arange(shard_count, dtype=jnp.int32)
    row = jnp.arange(row_count, dtype=jnp.int32)
    theta = -phase(
        (2 * shard[:, None] * shard[None, :])[None] + branch[:, None, None] * shard[None, None, :],
        2 * shard_count,
    )
    stage_a = jnp.stack([jnp.cos(theta), jnp.sin(theta)], axis=1)
    phi = -phase(
        (2 * shard[:, None] * row[None, :])[None] + branch[:, None, None] * row[None, :][None],
        2 * length,
    )
    twiddle = (jnp.cos(phi), jnp.sin(phi))
    psi = -phase(row[:, None] * row[None, :], row_count)
    cos_b, sin_b = jnp.cos(psi), jnp.sin(psi)
    stage_b = jnp.stack(
        [jnp.stack([cos_b, sin_b], axis=1), jnp.stack([-sin_b, cos_b], axis=1)]
    )
    stage_b_inv = jnp.stack(
        [jnp.stack([cos_b, -sin_b], axis=1), jnp.stack([sin_b, cos_b], axis=1)]
    )
    stage_a_inv = stage_a * (0.5 / length)
    return stage_a, twiddle, stage_b, stage_b_inv, stage_a_inv


def complex_scale(value, cos_part, sin_part, axis):
    real_part = lax.index_in_dim(value, 0, axis, keepdims=False)
    imag_part = lax.index_in_dim(value, 1, axis, keepdims=False)
    return jnp.stack(
        [real_part * cos_part - imag_part * sin_part, real_part * sin_part + imag_part * cos_part],
        axis=axis,
    )


def to_columns(rows, wire=jnp.float32):
    shard_count = lax.axis_size("seq")
    batch, row_count, _ = rows.shape
    columns = lax.all_to_all(
        jnp.swapaxes(rows, 1, 2).astype(wire), "seq", split_axis=1, concat_axis=2, tiled=True
    ).astype(jnp.float32)
    return columns.reshape(batch, columns.shape[1], shard_count, row_count)


def to_rows(columns, wire=jnp.float32, rim=0):
    batch, chan_count, shard_count, row_count = columns.shape
    if rim:
        ahead = jnp.concatenate(
            [columns[:, :, 1:, :rim], jnp.zeros_like(columns[:, :, :1, :rim])], axis=2
        )
        columns = jnp.concatenate([columns, ahead], axis=3)
    rows = lax.all_to_all(
        columns.astype(wire), "seq", split_axis=2, concat_axis=1, tiled=True
    ).astype(jnp.float32)
    return jnp.swapaxes(
        rows.reshape(batch, shard_count * chan_count, row_count + rim), 1, 2
    )


def forward_spectrum(columns, tables):
    stage_a, twiddle, stage_b, _, _ = tables
    spread = jnp.einsum("erkp,bcpm->bcerkm", stage_a, columns, precision=STAGE_A_PRECISION)
    spread = complex_scale(spread, twiddle[0], twiddle[1], 3)
    return jnp.einsum("bcerkm,rmsq->bceskq", spread, stage_b, precision=STAGE_B_PRECISION)


def inverse_spectrum(spectrum, tables):
    _, twiddle, _, stage_b_inv, stage_a_inv = tables
    spread = jnp.einsum("bceskq,sqrm->bcerkm", spectrum, stage_b_inv, precision=STAGE_B_PRECISION)
    spread = complex_scale(spread, twiddle[0], -twiddle[1], 3)
    return jnp.einsum("erkp,bcerkm->bcpm", stage_a_inv, spread, precision=STAGE_A_PRECISION)


def local(tokens, cotangent, in_weight, short_kernel, skip_gain, long_filter, out_weight):
    row_count = tokens.shape[0]
    tap_count = short_kernel.shape[0]
    shard_count = lax.axis_size("seq")
    tables = transform_tables(shard_count, row_count)
    filt_spec = forward_spectrum(to_columns(long_filter[None]), tables)
    width = tokens.shape[1]
    projected = 0.0
    for part, source in panel_parts(tokens):
        projected = projected + jnp.einsum(
            "td,jdc->jtc",
            part,
            lax.dynamic_slice_in_dim(in_weight, source * width, width, axis=1),
            preferred_element_type=jnp.float32,
        )
    grad_gated = 0.0
    for part, source in panel_parts(cotangent):
        grad_gated = grad_gated + lax.dot_general(
            part,
            lax.dynamic_slice_in_dim(out_weight, source * width, width, axis=1),
            (((1,), (1,)), ((), ())),
            preferred_element_type=jnp.float32,
        )
    projected = projected.astype(jnp.bfloat16)

    before = shifted(projected[:, row_count - (tap_count - 1) :, :], "seq", 1)
    extended = jnp.concatenate([before, projected], axis=1).astype(jnp.float32)
    filtered = short_kernel[0][:, None, :] * extended[:, tap_count - 1 :, :]
    for tap_index in range(1, tap_count):
        filtered = (
            filtered
            + short_kernel[tap_index][:, None, :]
            * extended[:, tap_count - 1 - tap_index : tap_count - 1 - tap_index + row_count, :]
        )
    gate_out, gate_in, value_path = (filtered[0], filtered[1], filtered[2])
    signal = value_path * gate_in
    grad_state = grad_gated * gate_out
    rim = tap_count - 1
    ahead = shifted(
        jnp.stack([gate_out[:rim], gate_in[:rim], value_path[:rim], grad_gated[:rim]]), "seq", -1
    )
    spectra = forward_spectrum(to_columns(jnp.stack([signal, grad_state]), WIRE), tables)
    filt_real, filt_imag = filt_spec[:, :, :, 0], filt_spec[:, :, :, 1]
    sig_real, sig_imag = spectra[0:1, :, :, 0], spectra[0:1, :, :, 1]
    grad_real, grad_imag = spectra[1:2, :, :, 0], spectra[1:2, :, :, 1]
    product = jnp.concatenate(
        [
            jnp.stack(
                [sig_real * filt_real - sig_imag * filt_imag, sig_real * filt_imag + sig_imag * filt_real],
                axis=3,
            ),
            jnp.stack(
                [grad_real * filt_real + grad_imag * filt_imag, grad_imag * filt_real - grad_real * filt_imag],
                axis=3,
            ),
        ]
    )
    convolved = to_rows(inverse_spectrum(product, tables), WIRE, rim)
    conv_state = convolved[0, :row_count] + skip_gain[None, :] * signal
    grad_signal = convolved[1, :row_count] + skip_gain[None, :] * grad_state
    conv_ahead = convolved[0, row_count:] + skip_gain[None, :] * (ahead[2] * ahead[1])
    grad_signal_ahead = convolved[1, row_count:] + skip_gain[None, :] * (ahead[3] * ahead[0])
    upstream_ahead = jnp.stack(
        [ahead[3] * conv_ahead, grad_signal_ahead * ahead[2], grad_signal_ahead * ahead[1]]
    )
    gated_state = (conv_state * gate_out).astype(jnp.bfloat16)
    block_out = panel_reduce_scatter(
        lambda dest: jnp.dot(
            gated_state,
            lax.dynamic_slice_in_dim(out_weight, dest * width, width, axis=1),
            preferred_element_type=jnp.float32,
        )
    )
    grad_gate_out = grad_gated * conv_state
    grad_value = grad_signal * gate_in
    grad_gate_in = grad_signal * value_path
    upstream = jnp.stack([grad_gate_out, grad_gate_in, grad_value])
    widened = jnp.concatenate([upstream, upstream_ahead], axis=1)
    grad_projected = short_kernel[0][:, None, :] * widened[:, :row_count, :]
    for tap_index in range(1, tap_count):
        grad_projected = (
            grad_projected
            + short_kernel[tap_index][:, None, :] * widened[:, tap_index : tap_index + row_count, :]
        )
    grad_projected = grad_projected.astype(jnp.bfloat16)
    token_grad = panel_reduce_scatter(
        lambda dest: jnp.einsum(
            "jtc,jdc->td",
            grad_projected,
            lax.dynamic_slice_in_dim(in_weight, dest * width, width, axis=1),
            preferred_element_type=jnp.float32,
        )
    )
    return (block_out, token_grad)


def solution(mesh):
    placed = (
        P("seq", "panel"),
        P("seq", "panel"),
        P(None, None, "panel"),
        P(None, None, "panel"),
        P("panel"),
        P("seq", "panel"),
        P("panel", None),
    )
    return jax.shard_map(
        local,
        mesh=mesh,
        in_specs=placed,
        out_specs=(P("seq", "panel"), P("seq", "panel")),
        check_vma=False,
    )
```

```python
import math

import jax
import jax.numpy as jnp
from jax import lax
from jax.sharding import PartitionSpec as P


STAGE_A_PRECISION = lax.Precision.HIGH
STAGE_B_PRECISION = lax.Precision.HIGH
WIRE = jnp.bfloat16


def shifted(value, axis, steps):
    count = lax.axis_size(axis)
    initial, last = (max(0, -steps), min(count, count - steps))
    return lax.ppermute(value, axis, [(source, source + steps) for source in range(initial, last)])


def panel_parts(value):
    count = lax.axis_size("panel")
    me = lax.axis_index("panel")
    parts = [(value, me)]
    for k in range(1, count):
        moved = lax.ppermute(value, "panel", [(i, (i + k) % count) for i in range(count)])
        parts.append((moved, (me + count - k) % count))
    return parts


def panel_reduce_scatter(block_of):
    count = lax.axis_size("panel")
    me = lax.axis_index("panel")
    total = block_of(me)
    for k in range(1, count):
        sent = block_of((me + k) % count).astype(jnp.bfloat16)
        total = total + lax.ppermute(
            sent, "panel", [(i, (i + k) % count) for i in range(count)]
        ).astype(jnp.float32)
    return total.astype(jnp.bfloat16)


def phase(numer, period):
    return (2.0 * math.pi / period) * (numer % period).astype(jnp.float32)


def transform_tables(shard_count, row_count):
    length = shard_count * row_count
    branch = jnp.arange(2, dtype=jnp.int32)
    shard = jnp.arange(shard_count, dtype=jnp.int32)
    row = jnp.arange(row_count, dtype=jnp.int32)
    theta = -phase(
        (2 * shard[:, None] * shard[None, :])[None] + branch[:, None, None] * shard[None, None, :],
        2 * shard_count,
    )
    stage_a = jnp.stack([jnp.cos(theta), jnp.sin(theta)], axis=1)
    phi = -phase(
        (2 * shard[:, None] * row[None, :])[None] + branch[:, None, None] * row[None, :][None],
        2 * length,
    )
    twiddle = (jnp.cos(phi), jnp.sin(phi))
    psi = -phase(row[:, None] * row[None, :], row_count)
    cos_b, sin_b = jnp.cos(psi), jnp.sin(psi)
    stage_b = jnp.stack(
        [jnp.stack([cos_b, sin_b], axis=1), jnp.stack([-sin_b, cos_b], axis=1)]
    )
    stage_b_inv = jnp.stack(
        [jnp.stack([cos_b, -sin_b], axis=1), jnp.stack([sin_b, cos_b], axis=1)]
    )
    stage_a_inv = stage_a * (0.5 / length)
    return stage_a, twiddle, stage_b, stage_b_inv, stage_a_inv


def complex_scale(value, cos_part, sin_part, axis):
    real_part = lax.index_in_dim(value, 0, axis, keepdims=False)
    imag_part = lax.index_in_dim(value, 1, axis, keepdims=False)
    return jnp.stack(
        [real_part * cos_part - imag_part * sin_part, real_part * sin_part + imag_part * cos_part],
        axis=axis,
    )


def to_columns(rows, wire=jnp.float32):
    shard_count = lax.axis_size("seq")
    batch, row_count, _ = rows.shape
    columns = lax.all_to_all(
        jnp.swapaxes(rows, 1, 2).astype(wire), "seq", split_axis=1, concat_axis=2, tiled=True
    ).astype(jnp.float32)
    return columns.reshape(batch, columns.shape[1], shard_count, row_count)


def to_rows(columns, wire=jnp.float32, rim=0):
    batch, chan_count, shard_count, row_count = columns.shape
    if rim:
        ahead = jnp.concatenate(
            [columns[:, :, 1:, :rim], jnp.zeros_like(columns[:, :, :1, :rim])], axis=2
        )
        columns = jnp.concatenate([columns, ahead], axis=3)
    rows = lax.all_to_all(
        columns.astype(wire), "seq", split_axis=2, concat_axis=1, tiled=True
    ).astype(jnp.float32)
    return jnp.swapaxes(
        rows.reshape(batch, shard_count * chan_count, row_count + rim), 1, 2
    )


def forward_spectrum(columns, tables):
    stage_a, twiddle, stage_b, _, _ = tables
    spread = jnp.einsum("erkp,bcpm->bcerkm", stage_a, columns, precision=STAGE_A_PRECISION)
    spread = complex_scale(spread, twiddle[0], twiddle[1], 3)
    return jnp.einsum("bcerkm,rmsq->bceskq", spread, stage_b, precision=STAGE_B_PRECISION)


def inverse_spectrum(spectrum, tables):
    _, twiddle, _, stage_b_inv, stage_a_inv = tables
    spread = jnp.einsum("bceskq,sqrm->bcerkm", spectrum, stage_b_inv, precision=STAGE_B_PRECISION)
    spread = complex_scale(spread, twiddle[0], -twiddle[1], 3)
    return jnp.einsum("erkp,bcerkm->bcpm", stage_a_inv, spread, precision=STAGE_A_PRECISION)


def local_body(tokens, cotangent, in_weight, short_kernel, skip_gain, long_filter, out_weight):
    row_count = tokens.shape[0]
    tap_count = short_kernel.shape[0]
    shard_count = lax.axis_size("seq")
    tables = transform_tables(shard_count, row_count)
    filt_spec = forward_spectrum(to_columns(long_filter[None]), tables)
    width = tokens.shape[1]
    projected = 0.0
    for part, source in panel_parts(tokens):
        projected = projected + jnp.einsum(
            "td,jdc->jtc",
            part,
            lax.dynamic_slice_in_dim(in_weight, source * width, width, axis=1),
            preferred_element_type=jnp.float32,
        )
    grad_gated = 0.0
    for part, source in panel_parts(cotangent):
        grad_gated = grad_gated + lax.dot_general(
            part,
            lax.dynamic_slice_in_dim(out_weight, source * width, width, axis=1),
            (((1,), (1,)), ((), ())),
            preferred_element_type=jnp.float32,
        )
    projected = projected.astype(jnp.bfloat16)

    before = shifted(projected[:, row_count - (tap_count - 1) :, :], "seq", 1)
    extended = jnp.concatenate([before, projected], axis=1).astype(jnp.float32)
    filtered = short_kernel[0][:, None, :] * extended[:, tap_count - 1 :, :]
    for tap_index in range(1, tap_count):
        filtered = (
            filtered
            + short_kernel[tap_index][:, None, :]
            * extended[:, tap_count - 1 - tap_index : tap_count - 1 - tap_index + row_count, :]
        )
    gate_out, gate_in, value_path = (filtered[0], filtered[1], filtered[2])
    signal = value_path * gate_in
    grad_state = grad_gated * gate_out
    rim = tap_count - 1
    ahead = shifted(
        jnp.stack([gate_out[:rim], gate_in[:rim], value_path[:rim], grad_gated[:rim]]),
        "seq",
        -1,
    )
    columns = to_columns(jnp.stack([signal, grad_state]), WIRE)
    spectra = forward_spectrum(columns, tables)
    filt_real, filt_imag = filt_spec[:, :, :, 0], filt_spec[:, :, :, 1]
    sig_real, sig_imag = spectra[0:1, :, :, 0], spectra[0:1, :, :, 1]
    grad_real, grad_imag = spectra[1:2, :, :, 0], spectra[1:2, :, :, 1]
    product = jnp.concatenate(
        [
            jnp.stack(
                [sig_real * filt_real - sig_imag * filt_imag, sig_real * filt_imag + sig_imag * filt_real],
                axis=3,
            ),
            jnp.stack(
                [grad_real * filt_real + grad_imag * filt_imag, grad_imag * filt_real - grad_real * filt_imag],
                axis=3,
            ),
        ]
    )
    convolved = to_rows(inverse_spectrum(product, tables), WIRE, rim)
    conv_state = convolved[0, :row_count] + skip_gain[None, :] * signal
    grad_signal = convolved[1, :row_count] + skip_gain[None, :] * grad_state
    conv_ahead = convolved[0, row_count:] + skip_gain[None, :] * (ahead[2] * ahead[1])
    grad_signal_ahead = convolved[1, row_count:] + skip_gain[None, :] * (ahead[3] * ahead[0])
    upstream_ahead = jnp.stack(
        [ahead[3] * conv_ahead, grad_signal_ahead * ahead[2], grad_signal_ahead * ahead[1]]
    )
    gated_state = (conv_state * gate_out).astype(jnp.bfloat16)
    block_out = panel_reduce_scatter(
        lambda dest: jnp.dot(
            gated_state,
            lax.dynamic_slice_in_dim(out_weight, dest * width, width, axis=1),
            preferred_element_type=jnp.float32,
        )
    )
    grad_gate_out = grad_gated * conv_state
    grad_value = grad_signal * gate_in
    grad_gate_in = grad_signal * value_path
    upstream = jnp.stack([grad_gate_out, grad_gate_in, grad_value])
    widened = jnp.concatenate([upstream, upstream_ahead], axis=1)
    grad_projected = short_kernel[0][:, None, :] * widened[:, :row_count, :]
    for tap_index in range(1, tap_count):
        grad_projected = (
            grad_projected
            + short_kernel[tap_index][:, None, :] * widened[:, tap_index : tap_index + row_count, :]
        )
    grad_projected = grad_projected.astype(jnp.bfloat16)
    token_grad = panel_reduce_scatter(
        lambda dest: jnp.einsum(
            "jtc,jdc->td",
            grad_projected,
            lax.dynamic_slice_in_dim(in_weight, dest * width, width, axis=1),
            preferred_element_type=jnp.float32,
        )
    )
    return (block_out, token_grad)


def solution(mesh):
    placed = (
        P("seq", "panel"),
        P("seq", "panel"),
        P(None, None, "panel"),
        P(None, None, "panel"),
        P("panel"),
        P("seq", "panel"),
        P("panel", None),
    )
    return jax.shard_map(
        local_body,
        mesh=mesh,
        in_specs=placed,
        out_specs=(P("seq", "panel"), P("seq", "panel")),
        check_vma=False,
    )
```

```python
import math

import jax
import jax.numpy as jnp
from jax import lax
from jax.sharding import PartitionSpec as P

HIGHEST = lax.Precision.HIGHEST
STAGE_A_PRECISION = lax.Precision.HIGH
STAGE_B_PRECISION = lax.Precision.HIGH
WIRE = jnp.bfloat16


def shifted(value, axis, steps):
    count = lax.axis_size(axis)
    initial, last = (max(0, -steps), min(count, count - steps))
    return lax.ppermute(value, axis, [(source, source + steps) for source in range(initial, last)])


def panel_parts(value):
    count = lax.axis_size("panel")
    me = lax.axis_index("panel")
    parts = [(value, me)]
    for k in range(1, count):
        moved = lax.ppermute(value, "panel", [(i, (i + k) % count) for i in range(count)])
        parts.append((moved, (me + count - k) % count))
    return parts


def panel_reduce_scatter(block_of):
    count = lax.axis_size("panel")
    blocks = jnp.stack([block_of(dest) for dest in range(count)]).astype(jnp.bfloat16)
    received = lax.all_to_all(blocks, "panel", 0, 0, tiled=True)
    return received.astype(jnp.float32).sum(axis=0).astype(jnp.bfloat16)


def phase(numer, period):
    return (2.0 * math.pi / period) * (numer % period).astype(jnp.float32)


def transform_tables(shard_count, row_count):
    length = shard_count * row_count
    branch = jnp.arange(2, dtype=jnp.int32)
    shard = jnp.arange(shard_count, dtype=jnp.int32)
    row = jnp.arange(row_count, dtype=jnp.int32)
    theta = -phase(
        (2 * shard[:, None] * shard[None, :])[None] + branch[:, None, None] * shard[None, None, :],
        2 * shard_count,
    )
    stage_a = jnp.stack([jnp.cos(theta), jnp.sin(theta)], axis=1)
    phi = -phase(
        (2 * shard[:, None] * row[None, :])[None] + branch[:, None, None] * row[None, :][None],
        2 * length,
    )
    twiddle = (jnp.cos(phi), jnp.sin(phi))
    psi = -phase(row[:, None] * row[None, :], row_count)
    cos_b, sin_b = jnp.cos(psi), jnp.sin(psi)
    stage_b = jnp.stack(
        [jnp.stack([cos_b, sin_b], axis=1), jnp.stack([-sin_b, cos_b], axis=1)]
    )
    stage_b_inv = jnp.stack(
        [jnp.stack([cos_b, -sin_b], axis=1), jnp.stack([sin_b, cos_b], axis=1)]
    )
    stage_a_inv = stage_a * (0.5 / length)
    return stage_a, twiddle, stage_b, stage_b_inv, stage_a_inv


def complex_scale(value, cos_part, sin_part, axis):
    real_part = lax.index_in_dim(value, 0, axis, keepdims=False)
    imag_part = lax.index_in_dim(value, 1, axis, keepdims=False)
    return jnp.stack(
        [real_part * cos_part - imag_part * sin_part, real_part * sin_part + imag_part * cos_part],
        axis=axis,
    )


def to_columns(rows, wire=jnp.float32):
    shard_count = lax.axis_size("seq")
    batch, row_count, _ = rows.shape
    columns = lax.all_to_all(
        jnp.swapaxes(rows, 1, 2).astype(wire), "seq", split_axis=1, concat_axis=2, tiled=True
    ).astype(jnp.float32)
    return columns.reshape(batch, columns.shape[1], shard_count, row_count)


def to_rows(columns, wire=jnp.float32):
    batch, chan_count, shard_count, row_count = columns.shape
    rows = lax.all_to_all(
        columns.astype(wire), "seq", split_axis=2, concat_axis=1, tiled=True
    ).astype(jnp.float32)
    return jnp.swapaxes(rows.reshape(batch, shard_count * chan_count, row_count), 1, 2)


def forward_spectrum(columns, tables):
    stage_a, twiddle, stage_b, _, _ = tables
    spread = jnp.einsum("erkp,bcpm->bcerkm", stage_a, columns, precision=STAGE_A_PRECISION)
    spread = complex_scale(spread, twiddle[0], twiddle[1], 3)
    return jnp.einsum("bcerkm,rmsq->bceskq", spread, stage_b, precision=STAGE_B_PRECISION)


def inverse_spectrum(spectrum, tables):
    _, twiddle, _, stage_b_inv, stage_a_inv = tables
    spread = jnp.einsum("bceskq,sqrm->bcerkm", spectrum, stage_b_inv, precision=STAGE_B_PRECISION)
    spread = complex_scale(spread, twiddle[0], -twiddle[1], 3)
    return jnp.einsum("erkp,bcerkm->bcpm", stage_a_inv, spread, precision=STAGE_A_PRECISION)


def local(tokens, cotangent, in_weight, short_kernel, skip_gain, long_filter, out_weight):
    row_count = tokens.shape[0]
    tap_count = short_kernel.shape[0]
    shard_count = lax.axis_size("seq")
    tables = transform_tables(shard_count, row_count)
    filt_spec = forward_spectrum(to_columns(long_filter[None]), tables)
    width = tokens.shape[1]
    projected = 0.0
    for part, source in panel_parts(tokens):
        projected = projected + jnp.einsum(
            "td,jdc->jtc",
            part,
            lax.dynamic_slice_in_dim(in_weight, source * width, width, axis=1),
            preferred_element_type=jnp.float32,
        )
    grad_gated = 0.0
    for part, source in panel_parts(cotangent):
        grad_gated = grad_gated + lax.dot_general(
            part,
            lax.dynamic_slice_in_dim(out_weight, source * width, width, axis=1),
            (((1,), (1,)), ((), ())),
            preferred_element_type=jnp.float32,
        )
    projected = projected.astype(jnp.bfloat16)

    before = shifted(projected[:, row_count - (tap_count - 1) :, :], "seq", 1)
    extended = jnp.concatenate([before, projected], axis=1).astype(jnp.float32)
    filtered = short_kernel[0][:, None, :] * extended[:, tap_count - 1 :, :]
    for tap_index in range(1, tap_count):
        filtered = (
            filtered
            + short_kernel[tap_index][:, None, :]
            * extended[:, tap_count - 1 - tap_index : tap_count - 1 - tap_index + row_count, :]
        )
    gate_out, gate_in, value_path = (filtered[0], filtered[1], filtered[2])
    signal = value_path * gate_in
    grad_state = grad_gated * gate_out
    spectra = forward_spectrum(to_columns(jnp.stack([signal, grad_state]), WIRE), tables)
    filt_real, filt_imag = filt_spec[:, :, :, 0], filt_spec[:, :, :, 1]
    sig_real, sig_imag = spectra[0:1, :, :, 0], spectra[0:1, :, :, 1]
    grad_real, grad_imag = spectra[1:2, :, :, 0], spectra[1:2, :, :, 1]
    product = jnp.concatenate(
        [
            jnp.stack(
                [sig_real * filt_real - sig_imag * filt_imag, sig_real * filt_imag + sig_imag * filt_real],
                axis=3,
            ),
            jnp.stack(
                [grad_real * filt_real + grad_imag * filt_imag, grad_imag * filt_real - grad_real * filt_imag],
                axis=3,
            ),
        ]
    )
    convolved = to_rows(inverse_spectrum(product, tables), WIRE)
    conv_state = convolved[0] + skip_gain[None, :] * signal
    grad_signal = convolved[1] + skip_gain[None, :] * grad_state
    gated_state = (conv_state * gate_out).astype(jnp.bfloat16)
    block_out = panel_reduce_scatter(
        lambda dest: jnp.dot(
            gated_state,
            lax.dynamic_slice_in_dim(out_weight, dest * width, width, axis=1),
            preferred_element_type=jnp.float32,
        )
    )
    grad_gate_out = grad_gated * conv_state
    grad_value = grad_signal * gate_in
    grad_gate_in = grad_signal * value_path
    upstream = jnp.stack([grad_gate_out, grad_gate_in, grad_value])
    after_rim = shifted(upstream[:, : tap_count - 1, :], "seq", -1)
    widened = jnp.concatenate([upstream, after_rim], axis=1)
    grad_projected = short_kernel[0][:, None, :] * widened[:, :row_count, :]
    for tap_index in range(1, tap_count):
        grad_projected = (
            grad_projected
            + short_kernel[tap_index][:, None, :] * widened[:, tap_index : tap_index + row_count, :]
        )
    grad_projected = grad_projected.astype(jnp.bfloat16)
    token_grad = panel_reduce_scatter(
        lambda dest: jnp.einsum(
            "jtc,jdc->td",
            grad_projected,
            lax.dynamic_slice_in_dim(in_weight, dest * width, width, axis=1),
            preferred_element_type=jnp.float32,
        )
    )
    return (block_out, token_grad)


def solution(mesh):
    placed = (
        P("seq", "panel"),
        P("seq", "panel"),
        P(None, None, "panel"),
        P(None, None, "panel"),
        P("panel"),
        P("seq", "panel"),
        P("panel", None),
    )
    return jax.shard_map(
        local,
        mesh=mesh,
        in_specs=placed,
        out_specs=(P("seq", "panel"), P("seq", "panel")),
        check_vma=False,
    )
```

```python
import math

import jax
import jax.numpy as jnp
from jax import lax
from jax.sharding import PartitionSpec as P

HIGHEST = lax.Precision.HIGHEST
STAGE_A_PRECISION = lax.Precision.HIGH
STAGE_B_PRECISION = lax.Precision.HIGH
WIRE = jnp.bfloat16


def shifted(value, axis, steps):
    count = lax.axis_size(axis)
    initial, last = (max(0, -steps), min(count, count - steps))
    return lax.ppermute(value, axis, [(source, source + steps) for source in range(initial, last)])


def panel_parts(value):
    count = lax.axis_size("panel")
    me = lax.axis_index("panel")
    parts = [(value, me)]
    for k in range(1, count):
        moved = lax.ppermute(value, "panel", [(i, (i + k) % count) for i in range(count)])
        parts.append((moved, (me + count - k) % count))
    return parts


def panel_reduce_scatter(block_of):
    count = lax.axis_size("panel")
    me = lax.axis_index("panel")
    total = block_of(me)
    for k in range(1, count):
        sent = block_of((me + k) % count).astype(jnp.bfloat16)
        total = total + lax.ppermute(
            sent, "panel", [(i, (i + k) % count) for i in range(count)]
        ).astype(jnp.float32)
    return total.astype(jnp.bfloat16)


def phase(numer, period):
    return (2.0 * math.pi / period) * (numer % period).astype(jnp.float32)


def transform_tables(shard_count, row_count):
    length = shard_count * row_count
    branch = jnp.arange(2, dtype=jnp.int32)
    shard = jnp.arange(shard_count, dtype=jnp.int32)
    row = jnp.arange(row_count, dtype=jnp.int32)
    theta = -phase(
        (2 * shard[:, None] * shard[None, :])[None] + branch[:, None, None] * shard[None, None, :],
        2 * shard_count,
    )
    stage_a = jnp.stack([jnp.cos(theta), jnp.sin(theta)], axis=1)
    phi = -phase(
        (2 * shard[:, None] * row[None, :])[None] + branch[:, None, None] * row[None, :][None],
        2 * length,
    )
    twiddle = (jnp.cos(phi), jnp.sin(phi))
    psi = -phase(row[:, None] * row[None, :], row_count)
    cos_b, sin_b = jnp.cos(psi), jnp.sin(psi)
    stage_b = jnp.stack(
        [jnp.stack([cos_b, sin_b], axis=1), jnp.stack([-sin_b, cos_b], axis=1)]
    )
    stage_a_inv = stage_a * (0.5 / length)
    return stage_a, twiddle, stage_b, stage_a_inv


def complex_scale(value, cos_part, sin_part, axis):
    real_part = lax.index_in_dim(value, 0, axis, keepdims=False)
    imag_part = lax.index_in_dim(value, 1, axis, keepdims=False)
    return jnp.stack(
        [real_part * cos_part - imag_part * sin_part, real_part * sin_part + imag_part * cos_part],
        axis=axis,
    )


def to_columns(rows, wire=jnp.float32):
    shard_count = lax.axis_size("seq")
    batch, row_count, _ = rows.shape
    columns = lax.all_to_all(
        jnp.swapaxes(rows, 1, 2).astype(wire), "seq", split_axis=1, concat_axis=2, tiled=True
    ).astype(jnp.float32)
    return columns.reshape(batch, columns.shape[1], shard_count, row_count)


def to_rows(columns, wire=jnp.float32):
    batch, chan_count, shard_count, row_count = columns.shape
    rows = lax.all_to_all(
        columns.astype(wire), "seq", split_axis=2, concat_axis=1, tiled=True
    ).astype(jnp.float32)
    return jnp.swapaxes(rows.reshape(batch, shard_count * chan_count, row_count), 1, 2)


def forward_spectrum(columns, tables):
    stage_a, twiddle, stage_b, _ = tables
    spread = jnp.einsum("erkp,bcpm->bcerkm", stage_a, columns, precision=STAGE_A_PRECISION)
    spread = complex_scale(spread, twiddle[0], twiddle[1], 3)
    return jnp.einsum("bcerkm,rmsq->bceskq", spread, stage_b, precision=STAGE_B_PRECISION)


def inverse_spectrum(spectrum, tables):
    _, twiddle, stage_b, stage_a_inv = tables
    spread = jnp.einsum("bceskq,rmsq->bcerkm", spectrum, stage_b, precision=STAGE_B_PRECISION)
    spread = complex_scale(spread, twiddle[0], -twiddle[1], 3)
    return jnp.einsum("erkp,bcerkm->bcpm", stage_a_inv, spread, precision=STAGE_A_PRECISION)


def local(tokens, cotangent, in_weight, short_kernel, skip_gain, long_filter, out_weight):
    row_count = tokens.shape[0]
    tap_count = short_kernel.shape[0]
    shard_count = lax.axis_size("seq")
    tables = transform_tables(shard_count, row_count)
    filt_spec = forward_spectrum(to_columns(long_filter[None]), tables)
    width = tokens.shape[1]
    projected = 0.0
    for part, source in panel_parts(tokens):
        projected = projected + jnp.einsum(
            "td,jdc->jtc",
            part,
            lax.dynamic_slice_in_dim(in_weight, source * width, width, axis=1),
            preferred_element_type=jnp.float32,
        )
    grad_gated = 0.0
    for part, source in panel_parts(cotangent):
        grad_gated = grad_gated + lax.dot_general(
            part,
            lax.dynamic_slice_in_dim(out_weight, source * width, width, axis=1),
            (((1,), (1,)), ((), ())),
            preferred_element_type=jnp.float32,
        )
    projected = projected.astype(jnp.bfloat16)

    before = shifted(projected[:, row_count - (tap_count - 1) :, :], "seq", 1)
    extended = jnp.concatenate([before, projected], axis=1).astype(jnp.float32)
    filtered = short_kernel[0][:, None, :] * extended[:, tap_count - 1 :, :]
    for tap_index in range(1, tap_count):
        filtered = (
            filtered
            + short_kernel[tap_index][:, None, :]
            * extended[:, tap_count - 1 - tap_index : tap_count - 1 - tap_index + row_count, :]
        )
    gate_out, gate_in, value_path = (filtered[0], filtered[1], filtered[2])
    signal = value_path * gate_in
    grad_state = grad_gated * gate_out
    spectra = forward_spectrum(to_columns(jnp.stack([signal, grad_state]), WIRE), tables)
    filt_real, filt_imag = filt_spec[:, :, :, 0], filt_spec[:, :, :, 1]
    sig_real, sig_imag = spectra[0:1, :, :, 0], spectra[0:1, :, :, 1]
    grad_real, grad_imag = spectra[1:2, :, :, 0], spectra[1:2, :, :, 1]
    product = jnp.concatenate(
        [
            jnp.stack(
                [sig_real * filt_real - sig_imag * filt_imag, sig_real * filt_imag + sig_imag * filt_real],
                axis=3,
            ),
            jnp.stack(
                [grad_real * filt_real + grad_imag * filt_imag, grad_imag * filt_real - grad_real * filt_imag],
                axis=3,
            ),
        ]
    )
    convolved = to_rows(inverse_spectrum(product, tables), WIRE)
    conv_state = convolved[0] + skip_gain[None, :] * signal
    grad_signal = convolved[1] + skip_gain[None, :] * grad_state
    gated_state = (conv_state * gate_out).astype(jnp.bfloat16)
    block_out = panel_reduce_scatter(
        lambda dest: jnp.dot(
            gated_state,
            lax.dynamic_slice_in_dim(out_weight, dest * width, width, axis=1),
            preferred_element_type=jnp.float32,
        )
    )
    grad_gate_out = grad_gated * conv_state
    grad_value = grad_signal * gate_in
    grad_gate_in = grad_signal * value_path
    upstream = jnp.stack([grad_gate_out, grad_gate_in, grad_value])
    after_rim = shifted(upstream[:, : tap_count - 1, :], "seq", -1)
    widened = jnp.concatenate([upstream, after_rim], axis=1)
    grad_projected = short_kernel[0][:, None, :] * widened[:, :row_count, :]
    for tap_index in range(1, tap_count):
        grad_projected = (
            grad_projected
            + short_kernel[tap_index][:, None, :] * widened[:, tap_index : tap_index + row_count, :]
        )
    grad_projected = grad_projected.astype(jnp.bfloat16)
    token_grad = panel_reduce_scatter(
        lambda dest: jnp.einsum(
            "jtc,jdc->td",
            grad_projected,
            lax.dynamic_slice_in_dim(in_weight, dest * width, width, axis=1),
            preferred_element_type=jnp.float32,
        )
    )
    return (block_out, token_grad)


def solution(mesh):
    placed = (
        P("seq", "panel"),
        P("seq", "panel"),
        P(None, None, "panel"),
        P(None, None, "panel"),
        P("panel"),
        P("seq", "panel"),
        P("panel", None),
    )
    return jax.shard_map(
        local,
        mesh=mesh,
        in_specs=placed,
        out_specs=(P("seq", "panel"), P("seq", "panel")),
        check_vma=False,
    )
```

```python
import math

import jax
import jax.numpy as jnp
import numpy as np
from jax import lax
from jax.sharding import PartitionSpec as P

HIGHEST = lax.Precision.HIGHEST
STAGE_A_PRECISION = lax.Precision.HIGH
STAGE_B_PRECISION = lax.Precision.HIGH
WIRE = jnp.bfloat16


def shifted(value, axis, steps):
    count = lax.axis_size(axis)
    initial, last = (max(0, -steps), min(count, count - steps))
    return lax.ppermute(value, axis, [(source, source + steps) for source in range(initial, last)])


def panel_parts(value):
    count = lax.axis_size("panel")
    me = lax.axis_index("panel")
    parts = [(value, me)]
    for k in range(1, count):
        moved = lax.ppermute(value, "panel", [(i, (i + k) % count) for i in range(count)])
        parts.append((moved, (me + count - k) % count))
    return parts


def panel_reduce_scatter(block_of):
    count = lax.axis_size("panel")
    me = lax.axis_index("panel")
    total = block_of(me)
    for k in range(1, count):
        sent = block_of((me + k) % count).astype(jnp.bfloat16)
        total = total + lax.ppermute(
            sent, "panel", [(i, (i + k) % count) for i in range(count)]
        ).astype(jnp.float32)
    return total.astype(jnp.bfloat16)


def phase(numer, period):
    return (2.0 * math.pi / period) * (numer % period).astype(jnp.float32)


def transform_tables(shard_count, row_count):
    length = shard_count * row_count
    branch = jnp.arange(2, dtype=jnp.int32)
    shard = jnp.arange(shard_count, dtype=jnp.int32)
    row = jnp.arange(row_count, dtype=jnp.int32)
    small_shard, small_row = np.arange(shard_count), np.arange(row_count)
    small_branch = np.arange(2)
    theta = (-2.0 * math.pi / (2 * shard_count)) * (
        (
            (2 * small_shard[:, None] * small_shard[None, :])[None]
            + small_branch[:, None, None] * small_shard[None, None, :]
        )
        % (2 * shard_count)
    )
    stage_a_np = np.stack([np.cos(theta), np.sin(theta)], axis=1)
    stage_a = jnp.asarray(stage_a_np, dtype=jnp.float32)
    phi = (-2.0 * math.pi / (2 * length)) * (
        (
            (2 * small_shard[:, None] * small_row[None, :])[None]
            + small_branch[:, None, None] * small_row[None, :][None]
        )
        % (2 * length)
    )
    twiddle = (jnp.asarray(np.cos(phi), jnp.float32), jnp.asarray(np.sin(phi), jnp.float32))
    psi = -phase(row[:, None] * row[None, :], row_count)
    cos_b, sin_b = jnp.cos(psi), jnp.sin(psi)
    stage_b = jnp.stack(
        [jnp.stack([cos_b, sin_b], axis=1), jnp.stack([-sin_b, cos_b], axis=1)]
    )
    stage_a_inv = jnp.asarray(stage_a_np * (0.5 / length), dtype=jnp.float32)
    return stage_a, twiddle, stage_b, stage_a_inv


def complex_scale(value, cos_part, sin_part, axis):
    real_part = lax.index_in_dim(value, 0, axis, keepdims=False)
    imag_part = lax.index_in_dim(value, 1, axis, keepdims=False)
    return jnp.stack(
        [real_part * cos_part - imag_part * sin_part, real_part * sin_part + imag_part * cos_part],
        axis=axis,
    )


def to_columns(rows, wire=jnp.float32):
    shard_count = lax.axis_size("seq")
    batch, row_count, _ = rows.shape
    columns = lax.all_to_all(
        jnp.swapaxes(rows, 1, 2).astype(wire), "seq", split_axis=1, concat_axis=2, tiled=True
    ).astype(jnp.float32)
    return columns.reshape(batch, columns.shape[1], shard_count, row_count)


def to_rows(columns, wire=jnp.float32):
    batch, chan_count, shard_count, row_count = columns.shape
    rows = lax.all_to_all(
        columns.astype(wire), "seq", split_axis=2, concat_axis=1, tiled=True
    ).astype(jnp.float32)
    return jnp.swapaxes(rows.reshape(batch, shard_count * chan_count, row_count), 1, 2)


def forward_spectrum(columns, tables):
    stage_a, twiddle, stage_b, _ = tables
    spread = jnp.einsum("erkp,bcpm->bcerkm", stage_a, columns, precision=STAGE_A_PRECISION)
    spread = complex_scale(spread, twiddle[0], twiddle[1], 3)
    return jnp.einsum("bcerkm,rmsq->bceskq", spread, stage_b, precision=STAGE_B_PRECISION)


def inverse_spectrum(spectrum, tables):
    _, twiddle, stage_b, stage_a_inv = tables
    spread = jnp.einsum("bceskq,rmsq->bcerkm", spectrum, stage_b, precision=STAGE_B_PRECISION)
    spread = complex_scale(spread, twiddle[0], -twiddle[1], 3)
    return jnp.einsum("erkp,bcerkm->bcpm", stage_a_inv, spread, precision=STAGE_A_PRECISION)


def local(tokens, cotangent, in_weight, short_kernel, skip_gain, long_filter, out_weight):
    row_count = tokens.shape[0]
    tap_count = short_kernel.shape[0]
    shard_count = lax.axis_size("seq")
    tables = transform_tables(shard_count, row_count)
    filt_spec = forward_spectrum(to_columns(long_filter[None]), tables)
    width = tokens.shape[1]
    projected = 0.0
    for part, source in panel_parts(tokens):
        projected = projected + jnp.einsum(
            "td,jdc->jtc",
            part,
            lax.dynamic_slice_in_dim(in_weight, source * width, width, axis=1),
            preferred_element_type=jnp.float32,
        )
    grad_gated = 0.0
    for part, source in panel_parts(cotangent):
        grad_gated = grad_gated + lax.dot_general(
            part,
            lax.dynamic_slice_in_dim(out_weight, source * width, width, axis=1),
            (((1,), (1,)), ((), ())),
            preferred_element_type=jnp.float32,
        )
    projected = projected.astype(jnp.bfloat16)

    before = shifted(projected[:, row_count - (tap_count - 1) :, :], "seq", 1)
    extended = jnp.concatenate([before, projected], axis=1).astype(jnp.float32)
    filtered = short_kernel[0][:, None, :] * extended[:, tap_count - 1 :, :]
    for tap_index in range(1, tap_count):
        filtered = (
            filtered
            + short_kernel[tap_index][:, None, :]
            * extended[:, tap_count - 1 - tap_index : tap_count - 1 - tap_index + row_count, :]
        )
    gate_out, gate_in, value_path = (filtered[0], filtered[1], filtered[2])
    signal = value_path * gate_in
    grad_state = grad_gated * gate_out
    spectra = forward_spectrum(to_columns(jnp.stack([signal, grad_state]), WIRE), tables)
    filt_real, filt_imag = filt_spec[:, :, :, 0], filt_spec[:, :, :, 1]
    sig_real, sig_imag = spectra[0:1, :, :, 0], spectra[0:1, :, :, 1]
    grad_real, grad_imag = spectra[1:2, :, :, 0], spectra[1:2, :, :, 1]
    product = jnp.concatenate(
        [
            jnp.stack(
                [sig_real * filt_real - sig_imag * filt_imag, sig_real * filt_imag + sig_imag * filt_real],
                axis=3,
            ),
            jnp.stack(
                [grad_real * filt_real + grad_imag * filt_imag, grad_imag * filt_real - grad_real * filt_imag],
                axis=3,
            ),
        ]
    )
    convolved = to_rows(inverse_spectrum(product, tables), WIRE)
    conv_state = convolved[0] + skip_gain[None, :] * signal
    grad_signal = convolved[1] + skip_gain[None, :] * grad_state
    gated_state = (conv_state * gate_out).astype(jnp.bfloat16)
    block_out = panel_reduce_scatter(
        lambda dest: jnp.dot(
            gated_state,
            lax.dynamic_slice_in_dim(out_weight, dest * width, width, axis=1),
            preferred_element_type=jnp.float32,
        )
    )
    grad_gate_out = grad_gated * conv_state
    grad_value = grad_signal * gate_in
    grad_gate_in = grad_signal * value_path
    upstream = jnp.stack([grad_gate_out, grad_gate_in, grad_value])
    after_rim = shifted(upstream[:, : tap_count - 1, :], "seq", -1)
    widened = jnp.concatenate([upstream, after_rim], axis=1)
    grad_projected = short_kernel[0][:, None, :] * widened[:, :row_count, :]
    for tap_index in range(1, tap_count):
        grad_projected = (
            grad_projected
            + short_kernel[tap_index][:, None, :] * widened[:, tap_index : tap_index + row_count, :]
        )
    grad_projected = grad_projected.astype(jnp.bfloat16)
    token_grad = panel_reduce_scatter(
        lambda dest: jnp.einsum(
            "jtc,jdc->td",
            grad_projected,
            lax.dynamic_slice_in_dim(in_weight, dest * width, width, axis=1),
            preferred_element_type=jnp.float32,
        )
    )
    return (block_out, token_grad)


def solution(mesh):
    placed = (
        P("seq", "panel"),
        P("seq", "panel"),
        P(None, None, "panel"),
        P(None, None, "panel"),
        P("panel"),
        P("seq", "panel"),
        P("panel", None),
    )
    return jax.shard_map(
        local,
        mesh=mesh,
        in_specs=placed,
        out_specs=(P("seq", "panel"), P("seq", "panel")),
        check_vma=False,
    )
```

```python
import math

import jax
import jax.numpy as jnp
import numpy as np
from jax import lax
from jax.sharding import PartitionSpec as P

HIGHEST = lax.Precision.HIGHEST
STAGE_A_PRECISION = lax.Precision.HIGH
STAGE_B_PRECISION = lax.Precision.HIGH
WIRE = jnp.bfloat16


def shifted(value, axis, steps):
    count = lax.axis_size(axis)
    initial, last = (max(0, -steps), min(count, count - steps))
    return lax.ppermute(value, axis, [(source, source + steps) for source in range(initial, last)])


def panel_parts(value):
    count = lax.axis_size("panel")
    me = lax.axis_index("panel")
    parts = [(value, me)]
    for k in range(1, count):
        moved = lax.ppermute(value, "panel", [(i, (i + k) % count) for i in range(count)])
        parts.append((moved, (me + count - k) % count))
    return parts


def panel_reduce_scatter(block_of):
    count = lax.axis_size("panel")
    me = lax.axis_index("panel")
    total = block_of(me)
    for k in range(1, count):
        sent = block_of((me + k) % count).astype(jnp.bfloat16)
        total = total + lax.ppermute(
            sent, "panel", [(i, (i + k) % count) for i in range(count)]
        ).astype(jnp.float32)
    return total.astype(jnp.bfloat16)


def phase(numer, period):
    return (2.0 * math.pi / period) * (numer % period).astype(jnp.float32)


def transform_tables(shard_count, row_count):
    length = shard_count * row_count
    branch = jnp.arange(2, dtype=jnp.int32)
    shard = jnp.arange(shard_count, dtype=jnp.int32)
    row = jnp.arange(row_count, dtype=jnp.int32)
    small_shard, small_row = np.arange(shard_count), np.arange(row_count)
    small_branch = np.arange(2)
    theta = (-2.0 * math.pi / (2 * shard_count)) * (
        (
            (2 * small_shard[:, None] * small_shard[None, :])[None]
            + small_branch[:, None, None] * small_shard[None, None, :]
        )
        % (2 * shard_count)
    )
    stage_a_np = np.stack([np.cos(theta), np.sin(theta)], axis=1)
    stage_a = jnp.asarray(stage_a_np, dtype=jnp.float32)
    phi = (-2.0 * math.pi / (2 * length)) * (
        (
            (2 * small_shard[:, None] * small_row[None, :])[None]
            + small_branch[:, None, None] * small_row[None, :][None]
        )
        % (2 * length)
    )
    twiddle = (jnp.asarray(np.cos(phi), jnp.float32), jnp.asarray(np.sin(phi), jnp.float32))
    base = (-2.0 * math.pi / row_count) * small_row
    index = (row[:, None] * row[None, :]) % row_count
    cos_b = jnp.take(jnp.asarray(np.cos(base), jnp.float32), index)
    sin_b = jnp.take(jnp.asarray(np.sin(base), jnp.float32), index)
    stage_b = jnp.stack(
        [jnp.stack([cos_b, sin_b], axis=1), jnp.stack([-sin_b, cos_b], axis=1)]
    )
    stage_a_inv = jnp.asarray(stage_a_np * (0.5 / length), dtype=jnp.float32)
    return stage_a, twiddle, stage_b, stage_a_inv


def complex_scale(value, cos_part, sin_part, axis):
    real_part = lax.index_in_dim(value, 0, axis, keepdims=False)
    imag_part = lax.index_in_dim(value, 1, axis, keepdims=False)
    return jnp.stack(
        [real_part * cos_part - imag_part * sin_part, real_part * sin_part + imag_part * cos_part],
        axis=axis,
    )


def to_columns(rows, wire=jnp.float32):
    shard_count = lax.axis_size("seq")
    batch, row_count, _ = rows.shape
    columns = lax.all_to_all(
        jnp.swapaxes(rows, 1, 2).astype(wire), "seq", split_axis=1, concat_axis=2, tiled=True
    ).astype(jnp.float32)
    return columns.reshape(batch, columns.shape[1], shard_count, row_count)


def to_rows(columns, wire=jnp.float32):
    batch, chan_count, shard_count, row_count = columns.shape
    rows = lax.all_to_all(
        columns.astype(wire), "seq", split_axis=2, concat_axis=1, tiled=True
    ).astype(jnp.float32)
    return jnp.swapaxes(rows.reshape(batch, shard_count * chan_count, row_count), 1, 2)


def forward_spectrum(columns, tables):
    stage_a, twiddle, stage_b, _ = tables
    spread = jnp.einsum("erkp,bcpm->bcerkm", stage_a, columns, precision=STAGE_A_PRECISION)
    spread = complex_scale(spread, twiddle[0], twiddle[1], 3)
    return jnp.einsum("bcerkm,rmsq->bceskq", spread, stage_b, precision=STAGE_B_PRECISION)


def inverse_spectrum(spectrum, tables):
    _, twiddle, stage_b, stage_a_inv = tables
    spread = jnp.einsum("bceskq,rmsq->bcerkm", spectrum, stage_b, precision=STAGE_B_PRECISION)
    spread = complex_scale(spread, twiddle[0], -twiddle[1], 3)
    return jnp.einsum("erkp,bcerkm->bcpm", stage_a_inv, spread, precision=STAGE_A_PRECISION)


def local(tokens, cotangent, in_weight, short_kernel, skip_gain, long_filter, out_weight):
    row_count = tokens.shape[0]
    tap_count = short_kernel.shape[0]
    shard_count = lax.axis_size("seq")
    tables = transform_tables(shard_count, row_count)
    filt_spec = forward_spectrum(to_columns(long_filter[None]), tables)
    width = tokens.shape[1]
    projected = 0.0
    for part, source in panel_parts(tokens):
        projected = projected + jnp.einsum(
            "td,jdc->jtc",
            part,
            lax.dynamic_slice_in_dim(in_weight, source * width, width, axis=1),
            preferred_element_type=jnp.float32,
        )
    grad_gated = 0.0
    for part, source in panel_parts(cotangent):
        grad_gated = grad_gated + lax.dot_general(
            part,
            lax.dynamic_slice_in_dim(out_weight, source * width, width, axis=1),
            (((1,), (1,)), ((), ())),
            preferred_element_type=jnp.float32,
        )
    projected = projected.astype(jnp.bfloat16)

    before = shifted(projected[:, row_count - (tap_count - 1) :, :], "seq", 1)
    extended = jnp.concatenate([before, projected], axis=1).astype(jnp.float32)
    filtered = short_kernel[0][:, None, :] * extended[:, tap_count - 1 :, :]
    for tap_index in range(1, tap_count):
        filtered = (
            filtered
            + short_kernel[tap_index][:, None, :]
            * extended[:, tap_count - 1 - tap_index : tap_count - 1 - tap_index + row_count, :]
        )
    gate_out, gate_in, value_path = (filtered[0], filtered[1], filtered[2])
    signal = value_path * gate_in
    grad_state = grad_gated * gate_out
    spectra = forward_spectrum(to_columns(jnp.stack([signal, grad_state]), WIRE), tables)
    filt_real, filt_imag = filt_spec[:, :, :, 0], filt_spec[:, :, :, 1]
    sig_real, sig_imag = spectra[0:1, :, :, 0], spectra[0:1, :, :, 1]
    grad_real, grad_imag = spectra[1:2, :, :, 0], spectra[1:2, :, :, 1]
    product = jnp.concatenate(
        [
            jnp.stack(
                [sig_real * filt_real - sig_imag * filt_imag, sig_real * filt_imag + sig_imag * filt_real],
                axis=3,
            ),
            jnp.stack(
                [grad_real * filt_real + grad_imag * filt_imag, grad_imag * filt_real - grad_real * filt_imag],
                axis=3,
            ),
        ]
    )
    convolved = to_rows(inverse_spectrum(product, tables), WIRE)
    conv_state = convolved[0] + skip_gain[None, :] * signal
    grad_signal = convolved[1] + skip_gain[None, :] * grad_state
    gated_state = (conv_state * gate_out).astype(jnp.bfloat16)
    block_out = panel_reduce_scatter(
        lambda dest: jnp.dot(
            gated_state,
            lax.dynamic_slice_in_dim(out_weight, dest * width, width, axis=1),
            preferred_element_type=jnp.float32,
        )
    )
    grad_gate_out = grad_gated * conv_state
    grad_value = grad_signal * gate_in
    grad_gate_in = grad_signal * value_path
    upstream = jnp.stack([grad_gate_out, grad_gate_in, grad_value])
    after_rim = shifted(upstream[:, : tap_count - 1, :], "seq", -1)
    widened = jnp.concatenate([upstream, after_rim], axis=1)
    grad_projected = short_kernel[0][:, None, :] * widened[:, :row_count, :]
    for tap_index in range(1, tap_count):
        grad_projected = (
            grad_projected
            + short_kernel[tap_index][:, None, :] * widened[:, tap_index : tap_index + row_count, :]
        )
    grad_projected = grad_projected.astype(jnp.bfloat16)
    token_grad = panel_reduce_scatter(
        lambda dest: jnp.einsum(
            "jtc,jdc->td",
            grad_projected,
            lax.dynamic_slice_in_dim(in_weight, dest * width, width, axis=1),
            preferred_element_type=jnp.float32,
        )
    )
    return (block_out, token_grad)


def solution(mesh):
    placed = (
        P("seq", "panel"),
        P("seq", "panel"),
        P(None, None, "panel"),
        P(None, None, "panel"),
        P("panel"),
        P("seq", "panel"),
        P("panel", None),
    )
    return jax.shard_map(
        local,
        mesh=mesh,
        in_specs=placed,
        out_specs=(P("seq", "panel"), P("seq", "panel")),
        check_vma=False,
    )
```
